32 devices in a mesh: leaf: 8 (over z, y), blk: 4 (over x, core).
Axes of the slice: x: 2, y: 2, z: 4, core: 2. Of those that a mesh axis runs over, the one named last changes fastest.
Arguments:
- parent_inverse: bfloat16 [8, 512, 512], P('leaf', None, 'blk'), as said below
- leaf_inverse: bfloat16 [112, 512, 512], P('leaf', 'blk'), as said below
- coupling: bfloat16 [112, 512, 512], P('leaf', 'blk'), may hold values from -0.25 to 0.25
- sensitivity: bfloat16 [112, 512, 512], P('leaf', 'blk'), may hold values from -0.25 to 0.25
- parent_of: int32 [112, 1], P('leaf'), may hold values from 0 to 7
- leaf_field: bfloat16 [112, 512], P('leaf'), may hold values from -6 to 6
- parent_field: bfloat16 [8, 512], P('leaf', 'blk'), may hold values from -6 to 6
Outputs:
- leaf_grad: float32 [112, 512], P('leaf', 'blk')
- coupling_grad: float32 [8, 512], P('leaf', 'blk')
The draws below stay inside these ranges and needn't reach their ends.
Inputs may be any that keep to these rules, and one draw needn't show every extreme that they name: `parent_of`: every one of the 8 separator supernodes is the parent of at least one leaf. `parent_inverse`: lower triangular with a positive diagonal. `leaf_inverse`: lower triangular with a positive diagonal.
All inputs are finite; a program needn't handle non-finite values.
Results may differ from the reference program's by a relative error of at most 0.0006.
Values may be sent and summed in bfloat16 or wider, within the bound.
No kernel may reach another device: no remote copies, remote signals or barrier semaphores. Data moves between devices by JAX's collectives and lax.ppermute only.
A program may use at most 128 MiB of HBM per device.

```python
import math
import jax
import jax.numpy as jnp
from jax import lax

W = 512
LEAVES = 112
NPAR = 8


def triangle_draw(key, number):
    diag_key, off_key = jax.random.split(key)
    row_index = lax.broadcasted_iota(jnp.int32, (number, W, W), 1)
    col_index = lax.broadcasted_iota(jnp.int32, (number, W, W), 2)
    diagonal = jnp.exp(jax.random.uniform(diag_key, (number, 1, W), jnp.float32, math.log(0.6), math.log(1.6)))
    lower = jax.random.normal(off_key, (number, W, W), jnp.float32) * (0.6 / math.sqrt(W))
    full = jnp.where(row_index > col_index, lower, 0.0) + jnp.where(row_index == col_index, diagonal, 0.0)
    return full.astype(jnp.bfloat16)


def draw_parent_inverse(key, part):
    return triangle_draw(jax.random.fold_in(key, 11), NPAR)


def draw_leaf_inverse(key, part):
    return triangle_draw(jax.random.fold_in(key, 23), LEAVES)


def steps_of(rng, extent, cuts, least, high):
    def one(axis_at, blocks):
        draws = jax.random.uniform(jax.random.fold_in(jax.random.fold_in(rng, 6), axis_at), (blocks,), jnp.float32, least / len(cuts), high / len(cuts))
        return jnp.repeat(jnp.exp(draws), extent[axis_at] // blocks).reshape((-1,) + (1,) * (len(extent) - axis_at - 1))

    gain = one(*cuts[0])
    for cut in cuts[1:]:
        gain = gain * one(*cut)
    return gain


def different_ones(stream_key, rows, count, top, lift):
    ranking = jax.random.permutation(jax.random.fold_in(stream_key, 1), count)
    favour = ranking
    for power in range(3):
        favour = favour * favour // count
    favour = favour * lift // count
    tickets = jax.random.randint(jax.random.fold_in(stream_key, 2), (rows, count), 0, 4096) + favour
    fixed_rows = jax.random.permutation(jax.random.fold_in(stream_key, 3), rows)[jnp.arange(count) % rows]
    tickets = jnp.where(jnp.arange(rows)[:, None] == fixed_rows[None, :], 1 << 14, tickets)
    merit = tickets * count + jnp.arange(count)
    return lax.top_k(merit.astype(jnp.int32), top)[1].astype(jnp.int32)


def scatter_about(stream_key, extent, scale, limit, cuts=(), kind=jnp.bfloat16):
    drawn = scale * jax.random.normal(stream_key, extent, jnp.float32)
    if cuts:
        drawn = drawn * steps_of(stream_key, extent, cuts, -0.22, 0.18)
    return jnp.clip(drawn, -limit, limit).astype(kind)


def setup_inputs(seed: int = 0) -> dict:
    key_of = jax.random.split(jax.random.key(seed), 8)
    return {
        "parent_inverse": draw_parent_inverse(jax.random.fold_in(key_of[7], 71), 0),
        "leaf_inverse": draw_leaf_inverse(jax.random.fold_in(key_of[7], 71), 0),
        "coupling": scatter_about(key_of[2], (LEAVES, W, W), W ** -0.5, 0.25, ((0, 8), (1, 4))),
        "sensitivity": scatter_about(key_of[3], (LEAVES, W, W), W ** -0.5, 0.25, ((0, 8), (1, 4))),
        "parent_of": different_ones(key_of[4], LEAVES, NPAR, 1, 2048),
        "leaf_field": scatter_about(key_of[5], (LEAVES, W), 1.0, 6.0, ((0, 8),)),
        "parent_field": scatter_about(key_of[6], (NPAR, W), 1.0, 6.0, ((0, 8), (1, 4))),
    }


def reference(parent_inverse, leaf_inverse, coupling, sensitivity, parent_of, leaf_field, parent_field):
    upper = parent_inverse.astype(jnp.float32)
    parent_cov = jnp.einsum('pki,pkj->pij', upper, upper).astype(jnp.bfloat16)

    def one_leaf(items):
        panel, inverse, sens, field, parent = items
        block = parent_cov[parent[0]]
        above = parent_field[parent[0]].astype(jnp.float32)
        mixed = jnp.dot(panel, inverse, preferred_element_type=jnp.float32).astype(jnp.bfloat16)
        cross = -jnp.dot(block, mixed, preferred_element_type=jnp.float32)
        cross_half = cross.astype(jnp.bfloat16)
        update = jnp.dot(panel.T, cross_half, preferred_element_type=jnp.float32)
        factor = inverse.astype(jnp.float32)
        diagonal = jnp.sum(factor * factor, 0) - jnp.sum(factor * update, 0)
        value = field.astype(jnp.float32)
        leaf_row = 0.5 * (diagonal - value * value)
        returned = jnp.sum(sens.astype(jnp.float32) * cross, 1) - above * jnp.dot(sens, field, preferred_element_type=jnp.float32)
        return leaf_row, returned

    leaf_grad, returned = lax.map(one_leaf, (coupling, leaf_inverse, sensitivity, leaf_field, parent_of))
    owners = (parent_of[:, 0:1] == jnp.arange(NPAR, dtype=jnp.int32)[None, :]).astype(jnp.float32)
    coupling_grad = jnp.dot(owners.T, returned, precision=lax.Precision.HIGHEST, preferred_element_type=jnp.float32)
    return leaf_grad, coupling_grad
```

```python
import jax
import jax.numpy as jnp
from jax import lax
from jax.sharding import PartitionSpec as P


def body(parent_inverse, leaf_inverse, coupling, sensitivity, parent_of, leaf_field, parent_field):
    count, share, width = coupling.shape
    offset = lax.axis_index("blk") * share
    cov_rows = jnp.einsum(
        "pkr,pkc->prc",
        parent_inverse,
        lax.all_gather(parent_inverse, "blk", axis=2, tiled=True),
        preferred_element_type=jnp.float32,
    ).astype(jnp.bfloat16)
    field_row = jnp.pad(parent_field, ((0, 0), (0, width - share)))[:, None, :]
    packed = jnp.concatenate([cov_rows, field_row], axis=1)
    pieces = lax.all_gather(packed, "leaf", axis=0, tiled=True)
    number = pieces.shape[0]
    parent_ids = parent_of[:, 0]
    position = jnp.clip(parent_ids, 0, number - 1)
    taken = jnp.take(pieces, position, axis=0)
    chosen_cov = taken[:, :share, :]
    chosen_field = taken[:, share, :share]
    full_inverse = lax.all_gather(leaf_inverse, "blk", axis=1, tiled=True)
    product = jnp.einsum(
        "lik,lkc->lic", coupling, full_inverse, preferred_element_type=jnp.float32
    )
    mixed = product.astype(jnp.bfloat16)
    cross = -jnp.einsum(
        "lrk,lkc->lrc",
        chosen_cov,
        lax.all_gather(mixed, "blk", axis=1, tiled=True),
        preferred_element_type=jnp.float32,
    )
    cross_half = cross.astype(jnp.bfloat16)
    factor = leaf_inverse.astype(jnp.float32)
    partial_diag = jnp.sum(factor * factor, 1) - jnp.sum(
        cross_half.astype(jnp.float32) * product, 1
    )
    diagonal = lax.psum_scatter(partial_diag, "blk", scatter_dimension=1, tiled=True)
    value = lax.dynamic_slice_in_dim(leaf_field, offset, share, 1).astype(jnp.float32)
    leaf_grad = 0.5 * (diagonal - value * value)
    returned = jnp.sum(sensitivity.astype(jnp.float32) * cross, 2) - chosen_field.astype(
        jnp.float32
    ) * jnp.einsum("lab,lb->la", sensitivity, leaf_field, preferred_element_type=jnp.float32)
    parent_total = lax.axis_size("leaf")
    owners = (
        parent_ids[:, None] == lax.broadcasted_iota(jnp.int32, (count, parent_total), 1)
    ).astype(jnp.float32)
    spread = jnp.einsum("lp,la->pa", owners, returned, precision=lax.Precision.HIGHEST)
    coupling_grad = lax.psum_scatter(spread, "leaf", scatter_dimension=0, tiled=True)
    return (leaf_grad, coupling_grad)


def solution(mesh):
    in_specs = (
        P("leaf", None, "blk"),
        P("leaf", "blk", None),
        P("leaf", "blk", None),
        P("leaf", "blk", None),
        P("leaf", None),
        P("leaf", None),
        P("leaf", "blk"),
    )
    out_specs = (P("leaf", "blk"), P("leaf", "blk"))
    return jax.shard_map(body, mesh=mesh, in_specs=in_specs, out_specs=out_specs, check_vma=False)
```

```python
import jax
import jax.numpy as jnp
from jax import lax
from jax.sharding import PartitionSpec as P


def swap(x, axis, mask):
    size = lax.axis_size(axis)
    return lax.ppermute(x, axis, [(i, i ^ mask) for i in range(size)])


def gather_blocks(x, axis):
    far = swap(x, axis, 2)
    near = swap(jnp.stack([x, far]), axis, 1)
    return [x, near[0], far, near[1]]


def shift(x, axis, step):
    size = lax.axis_size(axis)
    return lax.ppermute(x, axis, [(i, (i + step) % size) for i in range(size)])


def body(parent_inverse, leaf_inverse, coupling, sensitivity, parent_of, leaf_field, parent_field):
    count, share, width = coupling.shape
    me_blk = lax.axis_index("blk")
    me_leaf = lax.axis_index("leaf")
    number = lax.axis_size("leaf")
    offset = me_blk * share

    full_inverse = gather_blocks(leaf_inverse, "blk")
    upper_blocks = gather_blocks(parent_inverse, "blk")
    upper = jnp.take(jnp.stack(upper_blocks), jnp.arange(4) ^ me_blk, axis=0)
    upper = jnp.concatenate([upper[t] for t in range(4)], axis=2)
    cov_rows = jnp.einsum(
        "pkr,pkc->prc", parent_inverse, upper, preferred_element_type=jnp.float32
    ).astype(jnp.bfloat16)
    field_row = jnp.pad(parent_field, ((0, 0), (0, width - share)))[:, None, :]
    packed = jnp.concatenate([cov_rows, field_row], axis=1)[0]
    pieces = jnp.stack([packed] + [shift(packed, "leaf", s) for s in range(1, number)])
    parent_ids = parent_of[:, 0]
    position = (me_leaf - jnp.clip(parent_ids, 0, number - 1)) % number
    taken = jnp.take(pieces, position, axis=0)
    chosen_cov = taken[:, :share, :]
    chosen_field = taken[:, share, :share]

    def by_blocks(left, blocks):
        total = None
        for t, block in enumerate(blocks):
            cols = lax.dynamic_slice_in_dim(left, (me_blk ^ t) * share, share, 2)
            part = jnp.einsum("lik,lkc->lic", cols, block, preferred_element_type=jnp.float32)
            total = part if total is None else total + part
        return total

    product = by_blocks(coupling, full_inverse)
    mixed = product.astype(jnp.bfloat16)
    cross = -by_blocks(chosen_cov, gather_blocks(mixed, "blk"))
    cross_half = cross.astype(jnp.bfloat16)
    factor = leaf_inverse.astype(jnp.float32)
    partial_diag = jnp.sum(factor * factor, 1) - jnp.sum(
        cross_half.astype(jnp.float32) * product, 1
    )
    half = width // 2
    mine = lax.dynamic_slice_in_dim(partial_diag, (me_blk >> 1) * half, half, 1)
    other = lax.dynamic_slice_in_dim(partial_diag, (1 - (me_blk >> 1)) * half, half, 1)
    mine = mine + swap(other, "blk", 2)
    quarter = lax.dynamic_slice_in_dim(mine, (me_blk & 1) * share, share, 1)
    rest = lax.dynamic_slice_in_dim(mine, (1 - (me_blk & 1)) * share, share, 1)
    diagonal = quarter + swap(rest, "blk", 1)
    value = lax.dynamic_slice_in_dim(leaf_field, offset, share, 1).astype(jnp.float32)
    leaf_grad = 0.5 * (diagonal - value * value)
    returned = jnp.sum(sensitivity.astype(jnp.float32) * cross, 2) - chosen_field.astype(
        jnp.float32
    ) * jnp.einsum("lab,lb->la", sensitivity, leaf_field, preferred_element_type=jnp.float32)
    owners = (
        parent_ids[:, None] == lax.broadcasted_iota(jnp.int32, (count, number), 1)
    ).astype(jnp.float32)
    spread = jnp.einsum("lp,la->pa", owners, returned, precision=lax.Precision.HIGHEST)
    coupling_grad = lax.dynamic_slice_in_dim(spread, me_leaf, 1, 0)
    for s in range(1, number):
        row = lax.dynamic_slice_in_dim(spread, (me_leaf + s) % number, 1, 0)
        coupling_grad = coupling_grad + shift(row, "leaf", s)
    return (leaf_grad, coupling_grad)


def solution(mesh):
    in_specs = (
        P("leaf", None, "blk"),
        P("leaf", "blk", None),
        P("leaf", "blk", None),
        P("leaf", "blk", None),
        P("leaf", None),
        P("leaf", None),
        P("leaf", "blk"),
    )
    out_specs = (P("leaf", "blk"), P("leaf", "blk"))
    return jax.shard_map(body, mesh=mesh, in_specs=in_specs, out_specs=out_specs, check_vma=False)
```

```python
import jax
import jax.numpy as jnp
from jax import lax
from jax.sharding import PartitionSpec as P


def swap(x, axis, mask):
    size = lax.axis_size(axis)
    return lax.ppermute(x, axis, [(i, i ^ mask) for i in range(size)])


def gather_blocks(x, axis):
    far = swap(x, axis, 2)
    near = swap(jnp.stack([x, far]), axis, 1)
    return [x, near[0], far, near[1]]


def shift(x, axis, step):
    size = lax.axis_size(axis)
    return lax.ppermute(x, axis, [(i, (i + step) % size) for i in range(size)])


def body(parent_inverse, leaf_inverse, coupling, sensitivity, parent_of, leaf_field, parent_field):
    count, share, width = coupling.shape
    me_blk = lax.axis_index("blk")
    me_leaf = lax.axis_index("leaf")
    number = lax.axis_size("leaf")
    offset = me_blk * share

    upper_far = swap(parent_inverse, "blk", 2)
    local_inverse, upper_far = lax.optimization_barrier((leaf_inverse, upper_far))
    inverse_far = swap(local_inverse, "blk", 2)
    upper_near = swap(jnp.stack([parent_inverse, upper_far]), "blk", 1)
    upper_blocks = [parent_inverse, upper_near[0], upper_far, upper_near[1]]
    upper = jnp.take(jnp.stack(upper_blocks), jnp.arange(4) ^ me_blk, axis=0)
    upper = jnp.concatenate([upper[t] for t in range(4)], axis=2)
    cov_rows = jnp.einsum(
        "pkr,pkc->prc", parent_inverse, upper, preferred_element_type=jnp.float32
    ).astype(jnp.bfloat16)
    field_row = jnp.pad(parent_field, ((0, 0), (0, width - share)))[:, None, :]
    packed = jnp.concatenate([cov_rows, field_row], axis=1)[0]
    pieces = jnp.stack([packed] + [shift(packed, "leaf", s) for s in range(1, number)])
    near_in, pieces = lax.optimization_barrier((jnp.stack([local_inverse, inverse_far]), pieces))
    inverse_near = swap(near_in, "blk", 1)
    full_inverse = [leaf_inverse, inverse_near[0], inverse_far, inverse_near[1]]
    parent_ids = parent_of[:, 0]
    position = (me_leaf - jnp.clip(parent_ids, 0, number - 1)) % number
    taken = jnp.take(pieces, position, axis=0)
    chosen_cov = taken[:, :share, :]
    chosen_field = taken[:, share, :share]

    def by_blocks(left, blocks):
        total = None
        for t, block in enumerate(blocks):
            cols = lax.dynamic_slice_in_dim(left, (me_blk ^ t) * share, share, 2)
            part = jnp.einsum("lik,lkc->lic", cols, block, preferred_element_type=jnp.float32)
            total = part if total is None else total + part
        return total

    product = by_blocks(coupling, full_inverse)
    mixed = product.astype(jnp.bfloat16)
    cross = -by_blocks(chosen_cov, gather_blocks(mixed, "blk"))
    cross_half = cross.astype(jnp.bfloat16)
    factor = leaf_inverse.astype(jnp.float32)
    partial_diag = jnp.sum(factor * factor, 1) - jnp.sum(
        cross_half.astype(jnp.float32) * product, 1
    )
    half = width // 2
    mine = lax.dynamic_slice_in_dim(partial_diag, (me_blk >> 1) * half, half, 1)
    other = lax.dynamic_slice_in_dim(partial_diag, (1 - (me_blk >> 1)) * half, half, 1)
    mine = mine + swap(other, "blk", 2)
    quarter = lax.dynamic_slice_in_dim(mine, (me_blk & 1) * share, share, 1)
    rest = lax.dynamic_slice_in_dim(mine, (1 - (me_blk & 1)) * share, share, 1)
    diagonal = quarter + swap(rest, "blk", 1)
    value = lax.dynamic_slice_in_dim(leaf_field, offset, share, 1).astype(jnp.float32)
    leaf_grad = 0.5 * (diagonal - value * value)
    returned = jnp.sum(sensitivity.astype(jnp.float32) * cross, 2) - chosen_field.astype(
        jnp.float32
    ) * jnp.einsum("lab,lb->la", sensitivity, leaf_field, preferred_element_type=jnp.float32)
    owners = (
        parent_ids[:, None] == lax.broadcasted_iota(jnp.int32, (count, number), 1)
    ).astype(jnp.float32)
    spread = jnp.einsum("lp,la->pa", owners, returned, precision=lax.Precision.HIGHEST)
    coupling_grad = lax.dynamic_slice_in_dim(spread, me_leaf, 1, 0)
    for s in range(1, number):
        row = lax.dynamic_slice_in_dim(spread, (me_leaf + s) % number, 1, 0)
        coupling_grad = coupling_grad + shift(row, "leaf", s)
    return (leaf_grad, coupling_grad)


def solution(mesh):
    in_specs = (
        P("leaf", None, "blk"),
        P("leaf", "blk", None),
        P("leaf", "blk", None),
        P("leaf", "blk", None),
        P("leaf", None),
        P("leaf", None),
        P("leaf", "blk"),
    )
    out_specs = (P("leaf", "blk"), P("leaf", "blk"))
    return jax.shard_map(body, mesh=mesh, in_specs=in_specs, out_specs=out_specs, check_vma=False)
```

```python
import jax
import jax.numpy as jnp
from jax import lax
from jax.sharding import PartitionSpec as P


def swap(x, axis, mask):
    size = lax.axis_size(axis)
    return lax.ppermute(x, axis, [(i, i ^ mask) for i in range(size)])


def far(x):
    return swap(x, "blk", 2)


def near(x, far_x):
    both = swap(jnp.stack([x, far_x]), "blk", 1)
    return [x, both[0], far_x, both[1]]


def shift(x, axis, step):
    size = lax.axis_size(axis)
    return lax.ppermute(x, axis, [(i, (i + step) % size) for i in range(size)])


def tied(*values):
    return lax.optimization_barrier(values)


def reduce_to_owner(spread, me, number):
    if number & (number - 1):
        total = lax.dynamic_slice_in_dim(spread, me, 1, 0)
        for s in range(1, number):
            row = lax.dynamic_slice_in_dim(spread, (me + s) % number, 1, 0)
            total = total + shift(row, "leaf", s)
        return total
    current = spread
    mask = number // 2
    while mask:
        upper = (me & mask) // mask
        keep = lax.dynamic_slice_in_dim(current, upper * mask, mask, 0)
        give = lax.dynamic_slice_in_dim(current, (1 - upper) * mask, mask, 0)
        current = keep + swap(give, "leaf", mask)
        mask //= 2
    return current


def body(parent_inverse, leaf_inverse, coupling, sensitivity, parent_of, leaf_field, parent_field):
    count, share, width = coupling.shape
    me_blk = lax.axis_index("blk")
    me_leaf = lax.axis_index("leaf")
    number = lax.axis_size("leaf")
    offset = me_blk * share
    half_count = count // 2
    parts = [slice(0, half_count), slice(half_count, count)]

    def by_blocks(left, blocks):
        total = None
        for t, block in enumerate(blocks):
            cols = lax.dynamic_slice_in_dim(left, (me_blk ^ t) * share, share, 2)
            part = jnp.einsum("lik,lkc->lic", cols, block, preferred_element_type=jnp.float32)
            total = part if total is None else total + part
        return total

    upper_far = far(parent_inverse)
    inverse_a, upper_far = tied(leaf_inverse[parts[0]], upper_far)
    inverse_far_a = far(inverse_a)
    upper_blocks = near(parent_inverse, upper_far)
    upper = jnp.take(jnp.stack(upper_blocks), jnp.arange(4) ^ me_blk, axis=0)
    upper = jnp.concatenate([upper[t] for t in range(4)], axis=2)
    cov_rows = jnp.einsum(
        "pkr,pkc->prc", parent_inverse, upper, preferred_element_type=jnp.float32
    ).astype(jnp.bfloat16)
    field_row = jnp.pad(parent_field, ((0, 0), (0, width - share)))[:, None, :]
    packed = jnp.concatenate([cov_rows, field_row], axis=1)[0]
    pieces = jnp.stack([packed] + [shift(packed, "leaf", s) for s in range(1, number)])

    inverse_b, inverse_far_a = tied(leaf_inverse[parts[1]], inverse_far_a)
    inverse_far_b = far(inverse_b)
    product_a = by_blocks(coupling[parts[0]], near(inverse_a, inverse_far_a))
    mixed_a = product_a.astype(jnp.bfloat16)
    mixed_a, inverse_far_b, pieces = tied(mixed_a, inverse_far_b, pieces)
    mixed_far_a = far(mixed_a)
    product_b = by_blocks(coupling[parts[1]], near(inverse_b, inverse_far_b))
    mixed_b = product_b.astype(jnp.bfloat16)
    mixed_b, mixed_far_a = tied(mixed_b, mixed_far_a)
    mixed_far_b = far(mixed_b)

    parent_ids = parent_of[:, 0]
    position = (me_leaf - jnp.clip(parent_ids, 0, number - 1)) % number
    taken = jnp.take(pieces, position, axis=0)
    chosen_cov = taken[:, :share, :]
    chosen_field = taken[:, share, :share]

    cross_a = -by_blocks(chosen_cov[parts[0]], near(mixed_a, mixed_far_a))
    cross_b = -by_blocks(chosen_cov[parts[1]], near(mixed_b, mixed_far_b))
    cross = jnp.concatenate([cross_a, cross_b], axis=0)
    product = jnp.concatenate([product_a, product_b], axis=0)
    cross_half = cross.astype(jnp.bfloat16)
    factor = leaf_inverse.astype(jnp.float32)
    partial_diag = jnp.sum(factor * factor, 1) - jnp.sum(
        cross_half.astype(jnp.float32) * product, 1
    )
    half = width // 2
    mine = lax.dynamic_slice_in_dim(partial_diag, (me_blk >> 1) * half, half, 1)
    other = lax.dynamic_slice_in_dim(partial_diag, (1 - (me_blk >> 1)) * half, half, 1)
    mine = mine + swap(other, "blk", 2)
    quarter = lax.dynamic_slice_in_dim(mine, (me_blk & 1) * share, share, 1)
    rest = lax.dynamic_slice_in_dim(mine, (1 - (me_blk & 1)) * share, share, 1)
    diagonal = quarter + swap(rest, "blk", 1)
    value = lax.dynamic_slice_in_dim(leaf_field, offset, share, 1).astype(jnp.float32)
    leaf_grad = 0.5 * (diagonal - value * value)
    returned = jnp.sum(sensitivity.astype(jnp.float32) * cross, 2) - chosen_field.astype(
        jnp.float32
    ) * jnp.einsum("lab,lb->la", sensitivity, leaf_field, preferred_element_type=jnp.float32)
    owners = (
        parent_ids[:, None] == lax.broadcasted_iota(jnp.int32, (count, number), 1)
    ).astype(jnp.float32)
    spread = jnp.einsum("lp,la->pa", owners, returned, precision=lax.Precision.HIGHEST)
    coupling_grad = reduce_to_owner(spread, me_leaf, number)
    return (leaf_grad, coupling_grad)


def solution(mesh):
    in_specs = (
        P("leaf", None, "blk"),
        P("leaf", "blk", None),
        P("leaf", "blk", None),
        P("leaf", "blk", None),
        P("leaf", None),
        P("leaf", None),
        P("leaf", "blk"),
    )
    out_specs = (P("leaf", "blk"), P("leaf", "blk"))
    return jax.shard_map(body, mesh=mesh, in_specs=in_specs, out_specs=out_specs, check_vma=False)
```

```python
import jax
import jax.numpy as jnp
from jax import lax
from jax.sharding import PartitionSpec as P


def swap(x, axis, mask):
    size = lax.axis_size(axis)
    return lax.ppermute(x, axis, [(i, i ^ mask) for i in range(size)])


def far(x):
    return swap(x, "blk", 2)


def near(x, far_x):
    both = swap(jnp.stack([x, far_x]), "blk", 1)
    return [x, both[0], far_x, both[1]]


def shift(x, axis, step):
    size = lax.axis_size(axis)
    return lax.ppermute(x, axis, [(i, (i + step) % size) for i in range(size)])


def tied(*values):
    return lax.optimization_barrier(values)


def reduce_to_owner(spread, me, number):
    if number & (number - 1):
        total = lax.dynamic_slice_in_dim(spread, me, 1, 0)
        for s in range(1, number):
            row = lax.dynamic_slice_in_dim(spread, (me + s) % number, 1, 0)
            total = total + shift(row, "leaf", s)
        return total
    current = spread
    mask = number // 2
    while mask:
        upper = (me & mask) // mask
        keep = lax.dynamic_slice_in_dim(current, upper * mask, mask, 0)
        give = lax.dynamic_slice_in_dim(current, (1 - upper) * mask, mask, 0)
        current = keep + swap(give, "leaf", mask)
        mask //= 2
    return current


def body(parent_inverse, leaf_inverse, coupling, sensitivity, parent_of, leaf_field, parent_field):
    count, share, width = coupling.shape
    me_blk = lax.axis_index("blk")
    me_leaf = lax.axis_index("leaf")
    number = lax.axis_size("leaf")
    offset = me_blk * share
    half_count = count // 2
    parts = [slice(0, half_count), slice(half_count, count)]

    def by_blocks(left, blocks):
        total = None
        for t, block in enumerate(blocks):
            cols = lax.dynamic_slice_in_dim(left, (me_blk ^ t) * share, share, 2)
            part = jnp.einsum("lik,lkc->lic", cols, block, preferred_element_type=jnp.float32)
            total = part if total is None else total + part
        return total

    inverse_a = leaf_inverse[parts[0]]
    payload = jnp.concatenate([inverse_a, parent_inverse.reshape(1, share, width)], axis=0)
    payload_far = far(payload)
    inverse_far_a = payload_far[:half_count]
    upper_far = payload_far[half_count:].reshape(parent_inverse.shape)
    upper_blocks = near(parent_inverse, upper_far)
    upper = jnp.take(jnp.stack(upper_blocks), jnp.arange(4) ^ me_blk, axis=0)
    upper = jnp.concatenate([upper[t] for t in range(4)], axis=2)
    cov_rows = jnp.einsum(
        "pkr,pkc->prc", parent_inverse, upper, preferred_element_type=jnp.float32
    ).astype(jnp.bfloat16)
    field_row = jnp.pad(parent_field, ((0, 0), (0, width - share)))[:, None, :]
    packed = jnp.concatenate([cov_rows, field_row], axis=1)[0]
    pieces = jnp.stack([packed] + [shift(packed, "leaf", s) for s in range(1, number)])

    inverse_b, inverse_far_a = tied(leaf_inverse[parts[1]], inverse_far_a)
    inverse_far_b = far(inverse_b)
    product_a = by_blocks(coupling[parts[0]], near(inverse_a, inverse_far_a))
    mixed_a = product_a.astype(jnp.bfloat16)
    mixed_a, inverse_far_b = tied(mixed_a, inverse_far_b)
    mixed_far_a = far(mixed_a)
    product_b = by_blocks(coupling[parts[1]], near(inverse_b, inverse_far_b))
    mixed_b = product_b.astype(jnp.bfloat16)
    mixed_b, mixed_far_a, pieces = tied(mixed_b, mixed_far_a, pieces)
    mixed_far_b = far(mixed_b)

    parent_ids = parent_of[:, 0]
    position = (me_leaf - jnp.clip(parent_ids, 0, number - 1)) % number
    taken = jnp.take(pieces, position, axis=0)
    chosen_cov = taken[:, :share, :]
    chosen_field = taken[:, share, :share]

    cross_a = -by_blocks(chosen_cov[parts[0]], near(mixed_a, mixed_far_a))
    cross_b = -by_blocks(chosen_cov[parts[1]], near(mixed_b, mixed_far_b))
    cross = jnp.concatenate([cross_a, cross_b], axis=0)
    product = jnp.concatenate([product_a, product_b], axis=0)
    cross_half = cross.astype(jnp.bfloat16)
    factor = leaf_inverse.astype(jnp.float32)
    partial_diag = jnp.sum(factor * factor, 1) - jnp.sum(
        cross_half.astype(jnp.float32) * product, 1
    )
    half = width // 2
    mine = lax.dynamic_slice_in_dim(partial_diag, (me_blk >> 1) * half, half, 1)
    other = lax.dynamic_slice_in_dim(partial_diag, (1 - (me_blk >> 1)) * half, half, 1)
    mine = mine + swap(other, "blk", 2)
    quarter = lax.dynamic_slice_in_dim(mine, (me_blk & 1) * share, share, 1)
    rest = lax.dynamic_slice_in_dim(mine, (1 - (me_blk & 1)) * share, share, 1)
    diagonal = quarter + swap(rest, "blk", 1)
    value = lax.dynamic_slice_in_dim(leaf_field, offset, share, 1).astype(jnp.float32)
    leaf_grad = 0.5 * (diagonal - value * value)
    returned = jnp.sum(sensitivity.astype(jnp.float32) * cross, 2) - chosen_field.astype(
        jnp.float32
    ) * jnp.einsum("lab,lb->la", sensitivity, leaf_field, preferred_element_type=jnp.float32)
    owners = (
        parent_ids[:, None] == lax.broadcasted_iota(jnp.int32, (count, number), 1)
    ).astype(jnp.float32)
    spread = jnp.einsum("lp,la->pa", owners, returned, precision=lax.Precision.HIGHEST)
    coupling_grad = reduce_to_owner(spread, me_leaf, number)
    return (leaf_grad, coupling_grad)


def solution(mesh):
    in_specs = (
        P("leaf", None, "blk"),
        P("leaf", "blk", None),
        P("leaf", "blk", None),
        P("leaf", "blk", None),
        P("leaf", None),
        P("leaf", None),
        P("leaf", "blk"),
    )
    out_specs = (P("leaf", "blk"), P("leaf", "blk"))
    return jax.shard_map(body, mesh=mesh, in_specs=in_specs, out_specs=out_specs, check_vma=False)
```

```python
import jax
import jax.numpy as jnp
from jax import lax
from jax.sharding import PartitionSpec as P


def swap(x, axis, mask):
    size = lax.axis_size(axis)
    return lax.ppermute(x, axis, [(i, i ^ mask) for i in range(size)])


def far(x):
    return swap(x, "blk", 2)


def far_lower(x):
    me = lax.axis_index("blk")
    share, width = x.shape[-2], x.shape[-1]
    result = jnp.zeros_like(x)
    for source in range(lax.axis_size("blk")):
        target = source ^ 2
        cols = min(width, share * (source + 1))
        got = lax.ppermute(x[..., :cols], "blk", [(source, target)])
        got = jnp.pad(got, [(0, 0)] * (x.ndim - 1) + [(0, width - cols)])
        result = jnp.where(me == target, got, result)
    return result


def gather_leaf(x, number):
    if number & (number - 1):
        return jnp.stack([x] + [shift(x, "leaf", s) for s in range(1, number)])
    pieces = x[None]
    mask = 1
    while mask < number:
        pieces = jnp.concatenate([pieces, swap(pieces, "leaf", mask)], axis=0)
        mask *= 2
    return pieces


def near(x, far_x):
    both = swap(jnp.stack([x, far_x]), "blk", 1)
    return [x, both[0], far_x, both[1]]


def shift(x, axis, step):
    size = lax.axis_size(axis)
    return lax.ppermute(x, axis, [(i, (i + step) % size) for i in range(size)])


def tied(*values):
    return lax.optimization_barrier(values)


def reduce_to_owner(spread, me, number):
    if number & (number - 1):
        total = lax.dynamic_slice_in_dim(spread, me, 1, 0)
        for s in range(1, number):
            row = lax.dynamic_slice_in_dim(spread, (me + s) % number, 1, 0)
            total = total + shift(row, "leaf", s)
        return total
    current = spread
    mask = number // 2
    while mask:
        upper = (me & mask) // mask
        keep = lax.dynamic_slice_in_dim(current, upper * mask, mask, 0)
        give = lax.dynamic_slice_in_dim(current, (1 - upper) * mask, mask, 0)
        current = keep + swap(give, "leaf", mask)
        mask //= 2
    return current


def body(parent_inverse, leaf_inverse, coupling, sensitivity, parent_of, leaf_field, parent_field):
    count, share, width = coupling.shape
    me_blk = lax.axis_index("blk")
    me_leaf = lax.axis_index("leaf")
    number = lax.axis_size("leaf")
    offset = me_blk * share
    half_count = count // 2
    parts = [slice(0, half_count), slice(half_count, count)]

    def by_blocks(left, blocks):
        total = None
        for t, block in enumerate(blocks):
            cols = lax.dynamic_slice_in_dim(left, (me_blk ^ t) * share, share, 2)
            part = jnp.einsum("lik,lkc->lic", cols, block, preferred_element_type=jnp.float32)
            total = part if total is None else total + part
        return total

    upper_far = far(parent_inverse)
    inverse_a, upper_far = tied(leaf_inverse[parts[0]], upper_far)
    inverse_far_a = far_lower(inverse_a)
    upper_blocks = near(parent_inverse, upper_far)
    upper = jnp.take(jnp.stack(upper_blocks), jnp.arange(4) ^ me_blk, axis=0)
    upper = jnp.concatenate([upper[t] for t in range(4)], axis=2)
    cov_rows = jnp.einsum(
        "pkr,pkc->prc", parent_inverse, upper, preferred_element_type=jnp.float32
    ).astype(jnp.bfloat16)
    field_row = jnp.pad(parent_field, ((0, 0), (0, width - share)))[:, None, :]
    packed = jnp.concatenate([cov_rows, field_row], axis=1)[0]
    pieces = gather_leaf(packed, number)

    inverse_b, inverse_far_a = tied(leaf_inverse[parts[1]], inverse_far_a)
    inverse_far_b = far_lower(inverse_b)
    product_a = by_blocks(coupling[parts[0]], near(inverse_a, inverse_far_a))
    mixed_a = product_a.astype(jnp.bfloat16)
    mixed_a, inverse_far_b, pieces = tied(mixed_a, inverse_far_b, pieces)
    mixed_far_a = far(mixed_a)
    product_b = by_blocks(coupling[parts[1]], near(inverse_b, inverse_far_b))
    mixed_b = product_b.astype(jnp.bfloat16)
    mixed_b, mixed_far_a = tied(mixed_b, mixed_far_a)
    mixed_far_b = far(mixed_b)

    parent_ids = parent_of[:, 0]
    clipped = jnp.clip(parent_ids, 0, number - 1)
    if number & (number - 1):
        position = (me_leaf - clipped) % number
    else:
        position = me_leaf ^ clipped
    taken = jnp.take(pieces, position, axis=0)
    chosen_cov = taken[:, :share, :]
    chosen_field = taken[:, share, :share]

    cross_a = -by_blocks(chosen_cov[parts[0]], near(mixed_a, mixed_far_a))
    cross_b = -by_blocks(chosen_cov[parts[1]], near(mixed_b, mixed_far_b))
    cross = jnp.concatenate([cross_a, cross_b], axis=0)
    product = jnp.concatenate([product_a, product_b], axis=0)
    cross_half = cross.astype(jnp.bfloat16)
    factor = leaf_inverse.astype(jnp.float32)
    partial_diag = jnp.sum(factor * factor, 1) - jnp.sum(
        cross_half.astype(jnp.float32) * product, 1
    )
    half = width // 2
    mine = lax.dynamic_slice_in_dim(partial_diag, (me_blk >> 1) * half, half, 1)
    other = lax.dynamic_slice_in_dim(partial_diag, (1 - (me_blk >> 1)) * half, half, 1)
    mine = mine + swap(other, "blk", 2)
    quarter = lax.dynamic_slice_in_dim(mine, (me_blk & 1) * share, share, 1)
    rest = lax.dynamic_slice_in_dim(mine, (1 - (me_blk & 1)) * share, share, 1)
    diagonal = quarter + swap(rest, "blk", 1)
    value = lax.dynamic_slice_in_dim(leaf_field, offset, share, 1).astype(jnp.float32)
    leaf_grad = 0.5 * (diagonal - value * value)
    returned = jnp.sum(sensitivity.astype(jnp.float32) * cross, 2) - chosen_field.astype(
        jnp.float32
    ) * jnp.einsum("lab,lb->la", sensitivity, leaf_field, preferred_element_type=jnp.float32)
    owners = (
        parent_ids[:, None] == lax.broadcasted_iota(jnp.int32, (count, number), 1)
    ).astype(jnp.float32)
    spread = jnp.einsum("lp,la->pa", owners, returned, precision=lax.Precision.HIGHEST)
    coupling_grad = reduce_to_owner(spread, me_leaf, number)
    return (leaf_grad, coupling_grad)


def solution(mesh):
    in_specs = (
        P("leaf", None, "blk"),
        P("leaf", "blk", None),
        P("leaf", "blk", None),
        P("leaf", "blk", None),
        P("leaf", None),
        P("leaf", None),
        P("leaf", "blk"),
    )
    out_specs = (P("leaf", "blk"), P("leaf", "blk"))
    return jax.shard_map(body, mesh=mesh, in_specs=in_specs, out_specs=out_specs, check_vma=False)
```

```python
import jax
import jax.numpy as jnp
from jax import lax
from jax.sharding import PartitionSpec as P


def swap(x, axis, mask):
    size = lax.axis_size(axis)
    return lax.ppermute(x, axis, [(i, i ^ mask) for i in range(size)])


def far(x):
    return swap(x, "blk", 2)


def near(x, far_x):
    both = swap(jnp.stack([x, far_x]), "blk", 1)
    return [x, both[0], far_x, both[1]]


def shift(x, axis, step):
    size = lax.axis_size(axis)
    return lax.ppermute(x, axis, [(i, (i + step) % size) for i in range(size)])


def tied(*values):
    return lax.optimization_barrier(values)


def reduce_to_owner(spread, me, number):
    if number & (number - 1):
        total = lax.dynamic_slice_in_dim(spread, me, 1, 0)
        for s in range(1, number):
            row = lax.dynamic_slice_in_dim(spread, (me + s) % number, 1, 0)
            total = total + shift(row, "leaf", s)
        return total
    current = spread
    mask = number // 2
    while mask:
        upper = (me & mask) // mask
        keep = lax.dynamic_slice_in_dim(current, upper * mask, mask, 0)
        give = lax.dynamic_slice_in_dim(current, (1 - upper) * mask, mask, 0)
        current = keep + swap(give, "leaf", mask)
        mask //= 2
    return current


def body(parent_inverse, leaf_inverse, coupling, sensitivity, parent_of, leaf_field, parent_field):
    count, share, width = coupling.shape
    me_blk = lax.axis_index("blk")
    me_leaf = lax.axis_index("leaf")
    number = lax.axis_size("leaf")
    offset = me_blk * share
    half_count = (count * 5 + 7) // 8
    parts = [slice(0, half_count), slice(half_count, count)]

    def by_blocks(left, blocks):
        total = None
        for t, block in enumerate(blocks):
            cols = lax.dynamic_slice_in_dim(left, (me_blk ^ t) * share, share, 2)
            part = jnp.einsum("lik,lkc->lic", cols, block, preferred_element_type=jnp.float32)
            total = part if total is None else total + part
        return total

    upper_far = far(parent_inverse)
    inverse_a, upper_far = tied(leaf_inverse[parts[0]], upper_far)
    inverse_far_a = far(inverse_a)
    upper_blocks = near(parent_inverse, upper_far)
    upper = jnp.take(jnp.stack(upper_blocks), jnp.arange(4) ^ me_blk, axis=0)
    upper = jnp.concatenate([upper[t] for t in range(4)], axis=2)
    cov_rows = jnp.einsum(
        "pkr,pkc->prc", parent_inverse, upper, preferred_element_type=jnp.float32
    ).astype(jnp.bfloat16)
    field_row = jnp.pad(parent_field, ((0, 0), (0, width - share)))[:, None, :]
    packed = jnp.concatenate([cov_rows, field_row], axis=1)[0]
    pieces = jnp.stack([packed] + [shift(packed, "leaf", s) for s in range(1, number)])

    inverse_b, inverse_far_a = tied(leaf_inverse[parts[1]], inverse_far_a)
    inverse_far_b = far(inverse_b)
    product_a = by_blocks(coupling[parts[0]], near(inverse_a, inverse_far_a))
    mixed_a = product_a.astype(jnp.bfloat16)
    mixed_a, inverse_far_b, pieces = tied(mixed_a, inverse_far_b, pieces)
    mixed_far_a = far(mixed_a)
    product_b = by_blocks(coupling[parts[1]], near(inverse_b, inverse_far_b))
    mixed_b = product_b.astype(jnp.bfloat16)
    mixed_b, mixed_far_a = tied(mixed_b, mixed_far_a)
    mixed_far_b = far(mixed_b)

    parent_ids = parent_of[:, 0]
    position = (me_leaf - jnp.clip(parent_ids, 0, number - 1)) % number
    taken = jnp.take(pieces, position, axis=0)
    chosen_cov = taken[:, :share, :]
    chosen_field = taken[:, share, :share]

    cross_a = -by_blocks(chosen_cov[parts[0]], near(mixed_a, mixed_far_a))
    cross_b = -by_blocks(chosen_cov[parts[1]], near(mixed_b, mixed_far_b))
    cross = jnp.concatenate([cross_a, cross_b], axis=0)
    product = jnp.concatenate([product_a, product_b], axis=0)
    cross_half = cross.astype(jnp.bfloat16)
    factor = leaf_inverse.astype(jnp.float32)
    partial_diag = jnp.sum(factor * factor, 1) - jnp.sum(
        cross_half.astype(jnp.float32) * product, 1
    )
    half = width // 2
    mine = lax.dynamic_slice_in_dim(partial_diag, (me_blk >> 1) * half, half, 1)
    other = lax.dynamic_slice_in_dim(partial_diag, (1 - (me_blk >> 1)) * half, half, 1)
    mine = mine + swap(other, "blk", 2)
    quarter = lax.dynamic_slice_in_dim(mine, (me_blk & 1) * share, share, 1)
    rest = lax.dynamic_slice_in_dim(mine, (1 - (me_blk & 1)) * share, share, 1)
    diagonal = quarter + swap(rest, "blk", 1)
    value = lax.dynamic_slice_in_dim(leaf_field, offset, share, 1).astype(jnp.float32)
    leaf_grad = 0.5 * (diagonal - value * value)
    returned = jnp.sum(sensitivity.astype(jnp.float32) * cross, 2) - chosen_field.astype(
        jnp.float32
    ) * jnp.einsum("lab,lb->la", sensitivity, leaf_field, preferred_element_type=jnp.float32)
    owners = (
        parent_ids[:, None] == lax.broadcasted_iota(jnp.int32, (count, number), 1)
    ).astype(jnp.float32)
    spread = jnp.einsum("lp,la->pa", owners, returned, precision=lax.Precision.HIGHEST)
    coupling_grad = reduce_to_owner(spread, me_leaf, number)
    return (leaf_grad, coupling_grad)


def solution(mesh):
    in_specs = (
        P("leaf", None, "blk"),
        P("leaf", "blk", None),
        P("leaf", "blk", None),
        P("leaf", "blk", None),
        P("leaf", None),
        P("leaf", None),
        P("leaf", "blk"),
    )
    out_specs = (P("leaf", "blk"), P("leaf", "blk"))
    return jax.shard_map(body, mesh=mesh, in_specs=in_specs, out_specs=out_specs, check_vma=False)
```

```python
import jax
import jax.numpy as jnp
from jax import lax
from jax.sharding import PartitionSpec as P


def swap(x, axis, mask):
    size = lax.axis_size(axis)
    return lax.ppermute(x, axis, [(i, i ^ mask) for i in range(size)])


def far(x):
    return swap(x, "blk", 2)


def near(x, far_x):
    both = swap(jnp.stack([x, far_x]), "blk", 1)
    return [x, both[0], far_x, both[1]]


def shift(x, axis, step):
    size = lax.axis_size(axis)
    return lax.ppermute(x, axis, [(i, (i + step) % size) for i in range(size)])


def tied(*values):
    return lax.optimization_barrier(values)


def reduce_to_owner(spread, me, number):
    if number & (number - 1):
        total = lax.dynamic_slice_in_dim(spread, me, 1, 0)
        for s in range(1, number):
            row = lax.dynamic_slice_in_dim(spread, (me + s) % number, 1, 0)
            total = total + shift(row, "leaf", s)
        return total
    current = spread
    mask = number // 2
    while mask:
        upper = (me & mask) // mask
        keep = lax.dynamic_slice_in_dim(current, upper * mask, mask, 0)
        give = lax.dynamic_slice_in_dim(current, (1 - upper) * mask, mask, 0)
        current = keep + swap(give, "leaf", mask)
        mask //= 2
    return current


def body(parent_inverse, leaf_inverse, coupling, sensitivity, parent_of, leaf_field, parent_field):
    count, share, width = coupling.shape
    me_blk = lax.axis_index("blk")
    me_leaf = lax.axis_index("leaf")
    number = lax.axis_size("leaf")
    offset = me_blk * share
    half_count = count // 2
    parts = [slice(0, half_count), slice(half_count, count)]

    def by_blocks(left, blocks):
        total = None
        for t, block in enumerate(blocks):
            cols = lax.dynamic_slice_in_dim(left, (me_blk ^ t) * share, share, 2)
            part = jnp.einsum("lik,lkc->lic", cols, block, preferred_element_type=jnp.float32)
            total = part if total is None else total + part
        return total

    upper_far = far(parent_inverse)
    inverse_a, upper_far = tied(leaf_inverse[parts[0]], upper_far)
    inverse_far_a = far(inverse_a)
    upper_blocks = near(parent_inverse, upper_far)
    upper = jnp.take(jnp.stack(upper_blocks), jnp.arange(4) ^ me_blk, axis=0)
    upper = jnp.concatenate([upper[t] for t in range(4)], axis=2)
    cov_rows = jnp.einsum(
        "pkr,pkc->prc", parent_inverse, upper, preferred_element_type=jnp.float32
    ).astype(jnp.bfloat16)
    field_row = jnp.pad(parent_field, ((0, 0), (0, width - share)))[:, None, :]
    packed = jnp.concatenate([cov_rows, field_row], axis=1)[0]
    pieces = jnp.stack([packed] + [shift(packed, "leaf", s) for s in range(1, number)])

    inverse_b, inverse_far_a = tied(leaf_inverse[parts[1]], inverse_far_a)
    inverse_far_b = far(inverse_b)
    product_a = by_blocks(coupling[parts[0]], near(inverse_a, inverse_far_a))
    mixed_a = product_a.astype(jnp.bfloat16)
    mixed_a, inverse_far_b, pieces = tied(mixed_a, inverse_far_b, pieces)
    mixed_far_a = far(mixed_a)
    product_b = by_blocks(coupling[parts[1]], near(inverse_b, inverse_far_b))
    mixed_b = product_b.astype(jnp.bfloat16)
    mixed_b, mixed_far_a = tied(mixed_b, mixed_far_a)
    mixed_far_b = far(mixed_b)

    parent_ids = parent_of[:, 0]
    position = (me_leaf - jnp.clip(parent_ids, 0, number - 1)) % number
    taken = jnp.take(pieces, position, axis=0)
    chosen_cov = taken[:, :share, :]
    chosen_field = taken[:, share, :share]

    factor = leaf_inverse.astype(jnp.float32)
    field_terms = jnp.einsum("lab,lb->la", sensitivity, leaf_field, preferred_element_type=jnp.float32)
    half = width // 2

    def finish(part, cross_part, product_part):
        cross_half = cross_part.astype(jnp.bfloat16)
        local = factor[part]
        partial_diag = jnp.sum(local * local, 1) - jnp.sum(
            cross_half.astype(jnp.float32) * product_part, 1
        )
        mine = lax.dynamic_slice_in_dim(partial_diag, (me_blk >> 1) * half, half, 1)
        other = lax.dynamic_slice_in_dim(partial_diag, (1 - (me_blk >> 1)) * half, half, 1)
        mine = mine + swap(other, "blk", 2)
        quarter = lax.dynamic_slice_in_dim(mine, (me_blk & 1) * share, share, 1)
        rest = lax.dynamic_slice_in_dim(mine, (1 - (me_blk & 1)) * share, share, 1)
        diagonal = quarter + swap(rest, "blk", 1)
        returned = jnp.sum(sensitivity[part].astype(jnp.float32) * cross_part, 2) - chosen_field[
            part
        ].astype(jnp.float32) * field_terms[part]
        owners = (
            parent_ids[part, None] == lax.broadcasted_iota(jnp.int32, (returned.shape[0], number), 1)
        ).astype(jnp.float32)
        spread = jnp.einsum("lp,la->pa", owners, returned, precision=lax.Precision.HIGHEST)
        return diagonal, reduce_to_owner(spread, me_leaf, number)

    cross_a = -by_blocks(chosen_cov[parts[0]], near(mixed_a, mixed_far_a))
    diagonal_a, owned_a = finish(parts[0], cross_a, product_a)
    mixed_b, mixed_far_b, diagonal_a, owned_a = tied(mixed_b, mixed_far_b, diagonal_a, owned_a)
    cross_b = -by_blocks(chosen_cov[parts[1]], near(mixed_b, mixed_far_b))
    diagonal_b, owned_b = finish(parts[1], cross_b, product_b)
    diagonal = jnp.concatenate([diagonal_a, diagonal_b], axis=0)
    value = lax.dynamic_slice_in_dim(leaf_field, offset, share, 1).astype(jnp.float32)
    leaf_grad = 0.5 * (diagonal - value * value)
    coupling_grad = owned_a + owned_b
    return (leaf_grad, coupling_grad)


def solution(mesh):
    in_specs = (
        P("leaf", None, "blk"),
        P("leaf", "blk", None),
        P("leaf", "blk", None),
        P("leaf", "blk", None),
        P("leaf", None),
        P("leaf", None),
        P("leaf", "blk"),
    )
    out_specs = (P("leaf", "blk"), P("leaf", "blk"))
    return jax.shard_map(body, mesh=mesh, in_specs=in_specs, out_specs=out_specs, check_vma=False)
```

```python
import jax
import jax.numpy as jnp
from jax import lax
from jax.sharding import PartitionSpec as P


def swap(x, axis, mask):
    size = lax.axis_size(axis)
    return lax.ppermute(x, axis, [(i, i ^ mask) for i in range(size)])


def far(x):
    return swap(x, "blk", 2)


def near(x, far_x):
    both = swap(jnp.stack([x, far_x]), "blk", 1)
    return [x, both[0], far_x, both[1]]


def shift(x, axis, step):
    size = lax.axis_size(axis)
    return lax.ppermute(x, axis, [(i, (i + step) % size) for i in range(size)])


def tied(*values):
    return lax.optimization_barrier(values)


def reduce_to_owner(spread, me, number):
    if number & (number - 1):
        total = lax.dynamic_slice_in_dim(spread, me, 1, 0)
        for s in range(1, number):
            row = lax.dynamic_slice_in_dim(spread, (me + s) % number, 1, 0)
            total = total + shift(row, "leaf", s)
        return total
    current = spread
    mask = number // 2
    while mask:
        upper = (me & mask) // mask
        keep = lax.dynamic_slice_in_dim(current, upper * mask, mask, 0)
        give = lax.dynamic_slice_in_dim(current, (1 - upper) * mask, mask, 0)
        current = keep + swap(give, "leaf", mask)
        mask //= 2
    return current


def body(parent_inverse, leaf_inverse, coupling, sensitivity, parent_of, leaf_field, parent_field):
    count, share, width = coupling.shape
    me_blk = lax.axis_index("blk")
    me_leaf = lax.axis_index("leaf")
    number = lax.axis_size("leaf")
    offset = me_blk * share
    half_count = count // 2
    parts = [slice(0, half_count), slice(half_count, count)]

    def by_blocks(left, blocks):
        cols = jnp.concatenate(
            [lax.dynamic_slice_in_dim(left, (me_blk ^ t) * share, share, 2) for t in range(len(blocks))],
            axis=2,
        )
        right = jnp.concatenate(blocks, axis=1)
        return jnp.einsum("lik,lkc->lic", cols, right, preferred_element_type=jnp.float32)

    upper_far = far(parent_inverse)
    inverse_a, upper_far = tied(leaf_inverse[parts[0]], upper_far)
    inverse_far_a = far(inverse_a)
    upper_blocks = near(parent_inverse, upper_far)
    upper = jnp.take(jnp.stack(upper_blocks), jnp.arange(4) ^ me_blk, axis=0)
    upper = jnp.concatenate([upper[t] for t in range(4)], axis=2)
    cov_rows = jnp.einsum(
        "pkr,pkc->prc", parent_inverse, upper, preferred_element_type=jnp.float32
    ).astype(jnp.bfloat16)
    field_row = jnp.pad(parent_field, ((0, 0), (0, width - share)))[:, None, :]
    packed = jnp.concatenate([cov_rows, field_row], axis=1)[0]
    pieces = jnp.stack([packed] + [shift(packed, "leaf", s) for s in range(1, number)])

    inverse_b, inverse_far_a, pieces = tied(leaf_inverse[parts[1]], inverse_far_a, pieces)
    inverse_far_b = far(inverse_b)
    product_a = by_blocks(coupling[parts[0]], near(inverse_a, inverse_far_a))
    mixed_a = product_a.astype(jnp.bfloat16)
    mixed_a, inverse_far_b = tied(mixed_a, inverse_far_b)
    mixed_far_a = far(mixed_a)
    product_b = by_blocks(coupling[parts[1]], near(inverse_b, inverse_far_b))
    mixed_b = product_b.astype(jnp.bfloat16)
    mixed_b, mixed_far_a = tied(mixed_b, mixed_far_a)
    mixed_far_b = far(mixed_b)

    parent_ids = parent_of[:, 0]
    position = (me_leaf - jnp.clip(parent_ids, 0, number - 1)) % number
    taken = jnp.take(pieces, position, axis=0)
    chosen_cov = taken[:, :share, :]
    chosen_field = taken[:, share, :share]

    cross_a = -by_blocks(chosen_cov[parts[0]], near(mixed_a, mixed_far_a))
    cross_b = -by_blocks(chosen_cov[parts[1]], near(mixed_b, mixed_far_b))
    cross = jnp.concatenate([cross_a, cross_b], axis=0)
    product = jnp.concatenate([product_a, product_b], axis=0)
    cross_half = cross.astype(jnp.bfloat16)
    factor = leaf_inverse.astype(jnp.float32)
    partial_diag = jnp.sum(factor * factor, 1) - jnp.sum(
        cross_half.astype(jnp.float32) * product, 1
    )
    half = width // 2
    mine = lax.dynamic_slice_in_dim(partial_diag, (me_blk >> 1) * half, half, 1)
    other = lax.dynamic_slice_in_dim(partial_diag, (1 - (me_blk >> 1)) * half, half, 1)
    mine = mine + swap(other, "blk", 2)
    quarter = lax.dynamic_slice_in_dim(mine, (me_blk & 1) * share, share, 1)
    rest = lax.dynamic_slice_in_dim(mine, (1 - (me_blk & 1)) * share, share, 1)
    diagonal = quarter + swap(rest, "blk", 1)
    value = lax.dynamic_slice_in_dim(leaf_field, offset, share, 1).astype(jnp.float32)
    leaf_grad = 0.5 * (diagonal - value * value)
    returned = jnp.sum(sensitivity.astype(jnp.float32) * cross, 2) - chosen_field.astype(
        jnp.float32
    ) * jnp.einsum("lab,lb->la", sensitivity, leaf_field, preferred_element_type=jnp.float32)
    owners = (
        parent_ids[:, None] == lax.broadcasted_iota(jnp.int32, (count, number), 1)
    ).astype(jnp.float32)
    spread = jnp.einsum("lp,la->pa", owners, returned, precision=lax.Precision.HIGHEST)
    coupling_grad = reduce_to_owner(spread, me_leaf, number)
    return (leaf_grad, coupling_grad)


def solution(mesh):
    in_specs = (
        P("leaf", None, "blk"),
        P("leaf", "blk", None),
        P("leaf", "blk", None),
        P("leaf", "blk", None),
        P("leaf", None),
        P("leaf", None),
        P("leaf", "blk"),
    )
    out_specs = (P("leaf", "blk"), P("leaf", "blk"))
    return jax.shard_map(body, mesh=mesh, in_specs=in_specs, out_specs=out_specs, check_vma=False)
```

```python
import jax
import jax.numpy as jnp
from jax import lax
from jax.sharding import PartitionSpec as P


def swap(x, axis, mask):
    size = lax.axis_size(axis)
    return lax.ppermute(x, axis, [(i, i ^ mask) for i in range(size)])


def far(x):
    return swap(x, "blk", 2)


def near(x, far_x):
    both = swap(jnp.stack([x, far_x]), "blk", 1)
    return [x, both[0], far_x, both[1]]


def shift(x, axis, step):
    size = lax.axis_size(axis)
    return lax.ppermute(x, axis, [(i, (i + step) % size) for i in range(size)])


def tied(*values):
    return lax.optimization_barrier(values)


def reduce_to_owner(spread, me, number):
    if number & (number - 1):
        total = lax.dynamic_slice_in_dim(spread, me, 1, 0)
        for s in range(1, number):
            row = lax.dynamic_slice_in_dim(spread, (me + s) % number, 1, 0)
            total = total + shift(row, "leaf", s)
        return total
    current = spread
    mask = 1
    while mask < number:
        bit = (me & mask) // mask
        pairs = current.reshape(current.shape[0] // 2, 2, current.shape[1])
        keep = lax.dynamic_index_in_dim(pairs, bit, 1, keepdims=False)
        give = lax.dynamic_index_in_dim(pairs, 1 - bit, 1, keepdims=False)
        current = keep + swap(give, "leaf", mask)
        mask *= 2
    return current


def body(parent_inverse, leaf_inverse, coupling, sensitivity, parent_of, leaf_field, parent_field):
    count, share, width = coupling.shape
    me_blk = lax.axis_index("blk")
    me_leaf = lax.axis_index("leaf")
    number = lax.axis_size("leaf")
    offset = me_blk * share
    half_count = count // 2
    parts = [slice(0, half_count), slice(half_count, count)]

    def by_blocks(left, blocks):
        cols = jnp.concatenate(
            [lax.dynamic_slice_in_dim(left, (me_blk ^ t) * share, share, 2) for t in range(len(blocks))],
            axis=2,
        )
        right = jnp.concatenate(blocks, axis=1)
        return jnp.einsum("lik,lkc->lic", cols, right, preferred_element_type=jnp.float32)

    upper_far = far(parent_inverse)
    inverse_a, upper_far = tied(leaf_inverse[parts[0]], upper_far)
    inverse_far_a = far(inverse_a)
    upper_blocks = near(parent_inverse, upper_far)
    upper = jnp.take(jnp.stack(upper_blocks), jnp.arange(4) ^ me_blk, axis=0)
    upper = jnp.concatenate([upper[t] for t in range(4)], axis=2)
    cov_rows = jnp.einsum(
        "pkr,pkc->prc", parent_inverse, upper, preferred_element_type=jnp.float32
    ).astype(jnp.bfloat16)
    field_row = jnp.pad(parent_field, ((0, 0), (0, width - share)))[:, None, :]
    packed = jnp.concatenate([cov_rows, field_row], axis=1)[0]
    pieces = jnp.stack([packed] + [shift(packed, "leaf", s) for s in range(1, number)])

    inverse_b, inverse_far_a, pieces = tied(leaf_inverse[parts[1]], inverse_far_a, pieces)
    inverse_far_b = far(inverse_b)
    product_a = by_blocks(coupling[parts[0]], near(inverse_a, inverse_far_a))
    mixed_a = product_a.astype(jnp.bfloat16)
    mixed_a, inverse_far_b = tied(mixed_a, inverse_far_b)
    mixed_far_a = far(mixed_a)
    product_b = by_blocks(coupling[parts[1]], near(inverse_b, inverse_far_b))
    mixed_b = product_b.astype(jnp.bfloat16)
    mixed_b, mixed_far_a = tied(mixed_b, mixed_far_a)
    mixed_far_b = far(mixed_b)

    parent_ids = parent_of[:, 0]
    position = (me_leaf - jnp.clip(parent_ids, 0, number - 1)) % number
    taken = jnp.take(pieces, position, axis=0)
    chosen_cov = taken[:, :share, :]
    chosen_field = taken[:, share, :share]

    cross_a = -by_blocks(chosen_cov[parts[0]], near(mixed_a, mixed_far_a))
    cross_b = -by_blocks(chosen_cov[parts[1]], near(mixed_b, mixed_far_b))
    cross = jnp.concatenate([cross_a, cross_b], axis=0)
    product = jnp.concatenate([product_a, product_b], axis=0)
    cross_half = cross.astype(jnp.bfloat16)
    factor = leaf_inverse.astype(jnp.float32)
    partial_diag = jnp.sum(factor * factor, 1) - jnp.sum(
        cross_half.astype(jnp.float32) * product, 1
    )
    half = width // 2
    mine = lax.dynamic_slice_in_dim(partial_diag, (me_blk >> 1) * half, half, 1)
    other = lax.dynamic_slice_in_dim(partial_diag, (1 - (me_blk >> 1)) * half, half, 1)
    mine = mine + swap(other, "blk", 2)
    quarter = lax.dynamic_slice_in_dim(mine, (me_blk & 1) * share, share, 1)
    rest = lax.dynamic_slice_in_dim(mine, (1 - (me_blk & 1)) * share, share, 1)
    diagonal = quarter + swap(rest, "blk", 1)
    value = lax.dynamic_slice_in_dim(leaf_field, offset, share, 1).astype(jnp.float32)
    leaf_grad = 0.5 * (diagonal - value * value)
    returned = jnp.sum(sensitivity.astype(jnp.float32) * cross, 2) - chosen_field.astype(
        jnp.float32
    ) * jnp.einsum("lab,lb->la", sensitivity, leaf_field, preferred_element_type=jnp.float32)
    owners = (
        parent_ids[:, None] == lax.broadcasted_iota(jnp.int32, (count, number), 1)
    ).astype(jnp.float32)
    spread = jnp.einsum("lp,la->pa", owners, returned, precision=lax.Precision.HIGHEST)
    coupling_grad = reduce_to_owner(spread, me_leaf, number)
    return (leaf_grad, coupling_grad)


def solution(mesh):
    in_specs = (
        P("leaf", None, "blk"),
        P("leaf", "blk", None),
        P("leaf", "blk", None),
        P("leaf", "blk", None),
        P("leaf", None),
        P("leaf", None),
        P("leaf", "blk"),
    )
    out_specs = (P("leaf", "blk"), P("leaf", "blk"))
    return jax.shard_map(body, mesh=mesh, in_specs=in_specs, out_specs=out_specs, check_vma=False)
```

```python
import jax
import jax.numpy as jnp
from jax import lax
from jax.sharding import PartitionSpec as P


def swap(x, axis, mask):
    size = lax.axis_size(axis)
    return lax.ppermute(x, axis, [(i, i ^ mask) for i in range(size)])


def far(x):
    return swap(x, "blk", 2)


def near(x, far_x):
    both = swap(jnp.stack([x, far_x]), "blk", 1)
    return [x, both[0], far_x, both[1]]


def shift(x, axis, step):
    size = lax.axis_size(axis)
    return lax.ppermute(x, axis, [(i, (i + step) % size) for i in range(size)])


def tied(*values):
    return lax.optimization_barrier(values)


def reduce_to_owner(spread, me, number):
    if number & (number - 1):
        total = lax.dynamic_slice_in_dim(spread, me, 1, 0)
        for s in range(1, number):
            row = lax.dynamic_slice_in_dim(spread, (me + s) % number, 1, 0)
            total = total + shift(row, "leaf", s)
        return total
    current = spread
    mask = 1
    while mask < number:
        bit = (me & mask) // mask
        pairs = current.reshape(current.shape[0] // 2, 2, current.shape[1])
        keep = lax.dynamic_index_in_dim(pairs, bit, 1, keepdims=False)
        give = lax.dynamic_index_in_dim(pairs, 1 - bit, 1, keepdims=False)
        current = keep + swap(give, "leaf", mask)
        mask *= 2
    return current


def gather_leaf(x, number):
    if number & (number - 1):
        return jnp.stack([x] + [shift(x, "leaf", s) for s in range(1, number)])
    pieces = x[None]
    mask = 1
    while mask < number:
        pieces = jnp.concatenate([pieces, swap(pieces, "leaf", mask)], axis=0)
        mask *= 2
    return pieces


def body(parent_inverse, leaf_inverse, coupling, sensitivity, parent_of, leaf_field, parent_field):
    count, share, width = coupling.shape
    me_blk = lax.axis_index("blk")
    me_leaf = lax.axis_index("leaf")
    number = lax.axis_size("leaf")
    offset = me_blk * share
    owned = count // 2
    chip = me_blk >> 1
    mine_at = chip * owned
    theirs_at = (1 - chip) * owned

    def by_blocks(left, blocks):
        cols = jnp.concatenate(
            [lax.dynamic_slice_in_dim(left, (me_blk ^ t) * share, share, 2) for t in range(len(blocks))],
            axis=2,
        )
        right = jnp.concatenate(blocks, axis=1)
        return jnp.einsum("lik,lkc->lic", cols, right, preferred_element_type=jnp.float32)

    def ours(x):
        return lax.dynamic_slice_in_dim(x, mine_at, owned, 0)

    def theirs(x):
        return lax.dynamic_slice_in_dim(x, theirs_at, owned, 0)

    upper_far = far(parent_inverse)
    outgoing, upper_far = tied(jnp.stack([theirs(coupling), theirs(leaf_inverse)]), upper_far)
    incoming = far(outgoing)
    upper_blocks = near(parent_inverse, upper_far)
    upper = jnp.take(jnp.stack(upper_blocks), jnp.arange(4) ^ me_blk, axis=0)
    upper = jnp.concatenate([upper[t] for t in range(4)], axis=2)
    cov_rows = jnp.einsum(
        "pkr,pkc->prc", parent_inverse, upper, preferred_element_type=jnp.float32
    ).astype(jnp.bfloat16)
    field_row = jnp.pad(parent_field, ((0, 0), (0, width - share)))[:, None, :]
    packed = jnp.concatenate([cov_rows, field_row], axis=1)[0]
    packed = jnp.stack([packed, far(packed)])
    pieces = gather_leaf(packed, number)

    sens_out, incoming = tied(theirs(sensitivity), incoming)
    sens_in = far(sens_out)
    coupling_0, coupling_2 = ours(coupling), incoming[0]
    inverse_0, inverse_2 = ours(leaf_inverse), incoming[1]
    inverse_blocks = near(inverse_0, inverse_2)
    product_0 = by_blocks(coupling_0, inverse_blocks)
    product_2 = by_blocks(coupling_2, inverse_blocks)
    mixed_blocks = near(product_0.astype(jnp.bfloat16), product_2.astype(jnp.bfloat16))

    parent_ids = ours(parent_of)[:, 0]
    clipped = jnp.clip(parent_ids, 0, number - 1)
    if number & (number - 1):
        position = (me_leaf - clipped) % number
    else:
        position = me_leaf ^ clipped
    taken = jnp.take(pieces, position, axis=0)
    cross_0 = -by_blocks(taken[:, 0, :share, :], mixed_blocks)
    cross_2 = -by_blocks(taken[:, 1, :share, :], mixed_blocks)

    def diag_part(inverse_t, cross_t, product_t):
        factor = inverse_t.astype(jnp.float32)
        return jnp.sum(factor * factor, 1) - jnp.sum(
            cross_t.astype(jnp.bfloat16).astype(jnp.float32) * product_t, 1
        )

    partial_diag = diag_part(inverse_0, cross_0, product_0) + diag_part(inverse_2, cross_2, product_2)
    full_diag = partial_diag + swap(partial_diag, "blk", 1)
    own_cols = lax.dynamic_slice_in_dim(full_diag, offset, share, 1)
    their_cols = far(lax.dynamic_slice_in_dim(full_diag, (me_blk ^ 2) * share, share, 1))
    diagonal = jnp.where(
        chip == 0,
        jnp.concatenate([own_cols, their_cols], axis=0),
        jnp.concatenate([their_cols, own_cols], axis=0),
    )
    value = lax.dynamic_slice_in_dim(leaf_field, offset, share, 1).astype(jnp.float32)
    leaf_grad = 0.5 * (diagonal - value * value)

    field_terms_0 = jnp.einsum(
        "lab,lb->la", ours(sensitivity), ours(leaf_field), preferred_element_type=jnp.float32
    )
    field_terms_2 = jnp.einsum(
        "lab,lb->la", sens_in, ours(leaf_field), preferred_element_type=jnp.float32
    )
    returned_0 = jnp.sum(ours(sensitivity).astype(jnp.float32) * cross_0, 2) - taken[
        :, 0, share, :share
    ].astype(jnp.float32) * field_terms_0
    returned_2 = jnp.sum(sens_in.astype(jnp.float32) * cross_2, 2) - taken[
        :, 1, share, :share
    ].astype(jnp.float32) * field_terms_2
    owners = (
        parent_ids[:, None] == lax.broadcasted_iota(jnp.int32, (owned, number), 1)
    ).astype(jnp.float32)
    spread_0 = jnp.einsum("lp,la->pa", owners, returned_0, precision=lax.Precision.HIGHEST)
    spread_2 = jnp.einsum("lp,la->pa", owners, returned_2, precision=lax.Precision.HIGHEST)
    spread = spread_0 + far(spread_2)
    coupling_grad = reduce_to_owner(spread, me_leaf, number)
    return (leaf_grad, coupling_grad)


def solution(mesh):
    in_specs = (
        P("leaf", None, "blk"),
        P("leaf", "blk", None),
        P("leaf", "blk", None),
        P("leaf", "blk", None),
        P("leaf", None),
        P("leaf", None),
        P("leaf", "blk"),
    )
    out_specs = (P("leaf", "blk"), P("leaf", "blk"))
    return jax.shard_map(body, mesh=mesh, in_specs=in_specs, out_specs=out_specs, check_vma=False)
```

```python
import jax
import jax.numpy as jnp
from jax import lax
from jax.sharding import PartitionSpec as P


def swap(x, axis, mask):
    size = lax.axis_size(axis)
    return lax.ppermute(x, axis, [(i, i ^ mask) for i in range(size)])


def far(x):
    return swap(x, "blk", 2)


def near(x, far_x):
    both = swap(jnp.stack([x, far_x]), "blk", 1)
    return [x, both[0], far_x, both[1]]


def shift(x, axis, step):
    size = lax.axis_size(axis)
    return lax.ppermute(x, axis, [(i, (i + step) % size) for i in range(size)])


def tied(*values):
    return lax.optimization_barrier(values)


def reduce_to_owner(spread, me, number):
    if number & (number - 1):
        total = lax.dynamic_slice_in_dim(spread, me, 1, 0)
        for s in range(1, number):
            row = lax.dynamic_slice_in_dim(spread, (me + s) % number, 1, 0)
            total = total + shift(row, "leaf", s)
        return total
    current = spread
    mask = 1
    while mask < number:
        bit = (me & mask) // mask
        pairs = current.reshape(current.shape[0] // 2, 2, current.shape[1])
        keep = lax.dynamic_index_in_dim(pairs, bit, 1, keepdims=False)
        give = lax.dynamic_index_in_dim(pairs, 1 - bit, 1, keepdims=False)
        current = keep + swap(give, "leaf", mask)
        mask *= 2
    return current


def body(parent_inverse, leaf_inverse, coupling, sensitivity, parent_of, leaf_field, parent_field):
    count, share, width = coupling.shape
    me_blk = lax.axis_index("blk")
    me_leaf = lax.axis_index("leaf")
    number = lax.axis_size("leaf")
    offset = me_blk * share
    owned = count // 2
    chip = me_blk >> 1
    mine_at = chip * owned
    theirs_at = (1 - chip) * owned

    def by_blocks(left, blocks):
        cols = jnp.concatenate(
            [lax.dynamic_slice_in_dim(left, (me_blk ^ t) * share, share, 2) for t in range(len(blocks))],
            axis=2,
        )
        right = jnp.concatenate(blocks, axis=1)
        return jnp.einsum("lik,lkc->lic", cols, right, preferred_element_type=jnp.float32)

    def ours(x):
        return lax.dynamic_slice_in_dim(x, mine_at, owned, 0)

    def theirs(x):
        return lax.dynamic_slice_in_dim(x, theirs_at, owned, 0)

    upper_far = far(parent_inverse)
    outgoing, upper_far = tied(jnp.stack([theirs(coupling), theirs(leaf_inverse)]), upper_far)
    incoming = far(outgoing)
    upper_blocks = near(parent_inverse, upper_far)
    upper = jnp.take(jnp.stack(upper_blocks), jnp.arange(4) ^ me_blk, axis=0)
    upper = jnp.concatenate([upper[t] for t in range(4)], axis=2)
    cov_rows = jnp.einsum(
        "pkr,pkc->prc", parent_inverse, upper, preferred_element_type=jnp.float32
    ).astype(jnp.bfloat16)
    field_row = jnp.pad(parent_field, ((0, 0), (0, width - share)))[:, None, :]
    packed = jnp.concatenate([cov_rows, field_row], axis=1)[0]
    packed = jnp.stack([packed, far(packed)])
    pieces = jnp.stack([packed] + [shift(packed, "leaf", s) for s in range(1, number)])

    sens_out, incoming, pieces = tied(theirs(sensitivity), incoming, pieces)
    sens_in = far(sens_out)
    coupling_0, coupling_2 = ours(coupling), incoming[0]
    inverse_0, inverse_2 = ours(leaf_inverse), incoming[1]
    inverse_blocks = near(inverse_0, inverse_2)
    product_0 = by_blocks(coupling_0, inverse_blocks)
    product_2 = by_blocks(coupling_2, inverse_blocks)
    mixed_blocks = near(product_0.astype(jnp.bfloat16), product_2.astype(jnp.bfloat16))

    parent_ids = ours(parent_of)[:, 0]
    clipped = jnp.clip(parent_ids, 0, number - 1)
    position = (me_leaf - clipped) % number
    taken = jnp.take(pieces, position, axis=0)
    cross_0 = -by_blocks(taken[:, 0, :share, :], mixed_blocks)
    cross_2 = -by_blocks(taken[:, 1, :share, :], mixed_blocks)

    def diag_part(inverse_t, cross_t, product_t):
        factor = inverse_t.astype(jnp.float32)
        return jnp.sum(factor * factor, 1) - jnp.sum(
            cross_t.astype(jnp.bfloat16).astype(jnp.float32) * product_t, 1
        )

    partial_diag = diag_part(inverse_0, cross_0, product_0) + diag_part(inverse_2, cross_2, product_2)
    full_diag = partial_diag + swap(partial_diag, "blk", 1)
    own_cols = lax.dynamic_slice_in_dim(full_diag, offset, share, 1)
    their_cols = far(lax.dynamic_slice_in_dim(full_diag, (me_blk ^ 2) * share, share, 1))
    diagonal = jnp.where(
        chip == 0,
        jnp.concatenate([own_cols, their_cols], axis=0),
        jnp.concatenate([their_cols, own_cols], axis=0),
    )
    value = lax.dynamic_slice_in_dim(leaf_field, offset, share, 1).astype(jnp.float32)
    leaf_grad = 0.5 * (diagonal - value * value)

    field_terms_0 = jnp.einsum(
        "lab,lb->la", ours(sensitivity), ours(leaf_field), preferred_element_type=jnp.float32
    )
    field_terms_2 = jnp.einsum(
        "lab,lb->la", sens_in, ours(leaf_field), preferred_element_type=jnp.float32
    )
    returned_0 = jnp.sum(ours(sensitivity).astype(jnp.float32) * cross_0, 2) - taken[
        :, 0, share, :share
    ].astype(jnp.float32) * field_terms_0
    returned_2 = jnp.sum(sens_in.astype(jnp.float32) * cross_2, 2) - taken[
        :, 1, share, :share
    ].astype(jnp.float32) * field_terms_2
    owners = (
        parent_ids[:, None] == lax.broadcasted_iota(jnp.int32, (owned, number), 1)
    ).astype(jnp.float32)
    spread_0 = jnp.einsum("lp,la->pa", owners, returned_0, precision=lax.Precision.HIGHEST)
    spread_2 = jnp.einsum("lp,la->pa", owners, returned_2, precision=lax.Precision.HIGHEST)
    spread = spread_0 + far(spread_2)
    coupling_grad = reduce_to_owner(spread, me_leaf, number)
    return (leaf_grad, coupling_grad)


def solution(mesh):
    in_specs = (
        P("leaf", None, "blk"),
        P("leaf", "blk", None),
        P("leaf", "blk", None),
        P("leaf", "blk", None),
        P("leaf", None),
        P("leaf", None),
        P("leaf", "blk"),
    )
    out_specs = (P("leaf", "blk"), P("leaf", "blk"))
    return jax.shard_map(body, mesh=mesh, in_specs=in_specs, out_specs=out_specs, check_vma=False)
```

```python
import jax
import jax.numpy as jnp
from jax import lax
from jax.sharding import PartitionSpec as P


def swap(x, axis, mask):
    size = lax.axis_size(axis)
    return lax.ppermute(x, axis, [(i, i ^ mask) for i in range(size)])


def far(x):
    return swap(x, "blk", 2)


def near(x, far_x):
    both = swap(jnp.stack([x, far_x]), "blk", 1)
    return [x, both[0], far_x, both[1]]


def shift(x, axis, step):
    size = lax.axis_size(axis)
    return lax.ppermute(x, axis, [(i, (i + step) % size) for i in range(size)])


def tied(*values):
    return lax.optimization_barrier(values)


def reduce_to_owner(spread, me, number):
    if number & (number - 1):
        total = lax.dynamic_slice_in_dim(spread, me, 1, 0)
        for s in range(1, number):
            row = lax.dynamic_slice_in_dim(spread, (me + s) % number, 1, 0)
            total = total + shift(row, "leaf", s)
        return total
    current = spread
    mask = 1
    while mask < number:
        bit = (me & mask) // mask
        pairs = current.reshape(current.shape[0] // 2, 2, current.shape[1])
        keep = lax.dynamic_index_in_dim(pairs, bit, 1, keepdims=False)
        give = lax.dynamic_index_in_dim(pairs, 1 - bit, 1, keepdims=False)
        current = keep + swap(give, "leaf", mask)
        mask *= 2
    return current


def body(parent_inverse, leaf_inverse, coupling, sensitivity, parent_of, leaf_field, parent_field):
    count, share, width = coupling.shape
    me_blk = lax.axis_index("blk")
    me_leaf = lax.axis_index("leaf")
    number = lax.axis_size("leaf")
    offset = me_blk * share
    owned = count // 2
    chip = me_blk >> 1
    mine_at = chip * owned
    theirs_at = (1 - chip) * owned

    def by_blocks(left, blocks):
        cols = jnp.concatenate(
            [lax.dynamic_slice_in_dim(left, (me_blk ^ t) * share, share, 2) for t in range(len(blocks))],
            axis=2,
        )
        right = jnp.concatenate(blocks, axis=1)
        return jnp.einsum("lik,lkc->lic", cols, right, preferred_element_type=jnp.float32)

    def ours(x):
        return lax.dynamic_slice_in_dim(x, mine_at, owned, 0)

    def theirs(x):
        return lax.dynamic_slice_in_dim(x, theirs_at, owned, 0)

    upper_far = far(parent_inverse)
    outgoing, upper_far = tied(
        jnp.stack([theirs(coupling), theirs(leaf_inverse), theirs(sensitivity)]), upper_far
    )
    incoming = far(outgoing)
    upper_blocks = near(parent_inverse, upper_far)
    upper = jnp.take(jnp.stack(upper_blocks), jnp.arange(4) ^ me_blk, axis=0)
    upper = jnp.concatenate([upper[t] for t in range(4)], axis=2)
    cov_rows = jnp.einsum(
        "pkr,pkc->prc", parent_inverse, upper, preferred_element_type=jnp.float32
    ).astype(jnp.bfloat16)
    field_row = jnp.pad(parent_field, ((0, 0), (0, width - share)))[:, None, :]
    packed = jnp.concatenate([cov_rows, field_row], axis=1)[0]
    packed = jnp.stack([packed, far(packed)])
    pieces = jnp.stack([packed] + [shift(packed, "leaf", s) for s in range(1, number)])

    incoming, pieces = tied(incoming, pieces)
    sens_in = incoming[2]
    coupling_0, coupling_2 = ours(coupling), incoming[0]
    inverse_0, inverse_2 = ours(leaf_inverse), incoming[1]
    inverse_blocks = near(inverse_0, inverse_2)
    product_0 = by_blocks(coupling_0, inverse_blocks)
    product_2 = by_blocks(coupling_2, inverse_blocks)
    mixed_blocks = near(product_0.astype(jnp.bfloat16), product_2.astype(jnp.bfloat16))

    parent_ids = ours(parent_of)[:, 0]
    clipped = jnp.clip(parent_ids, 0, number - 1)
    position = (me_leaf - clipped) % number
    taken = jnp.take(pieces, position, axis=0)
    cross_0 = -by_blocks(taken[:, 0, :share, :], mixed_blocks)
    cross_2 = -by_blocks(taken[:, 1, :share, :], mixed_blocks)

    def diag_part(inverse_t, cross_t, product_t):
        factor = inverse_t.astype(jnp.float32)
        return jnp.sum(factor * factor, 1) - jnp.sum(
            cross_t.astype(jnp.bfloat16).astype(jnp.float32) * product_t, 1
        )

    partial_diag = diag_part(inverse_0, cross_0, product_0) + diag_part(inverse_2, cross_2, product_2)
    full_diag = partial_diag + swap(partial_diag, "blk", 1)
    own_cols = lax.dynamic_slice_in_dim(full_diag, offset, share, 1)
    their_cols = far(lax.dynamic_slice_in_dim(full_diag, (me_blk ^ 2) * share, share, 1))
    diagonal = jnp.where(
        chip == 0,
        jnp.concatenate([own_cols, their_cols], axis=0),
        jnp.concatenate([their_cols, own_cols], axis=0),
    )
    value = lax.dynamic_slice_in_dim(leaf_field, offset, share, 1).astype(jnp.float32)
    leaf_grad = 0.5 * (diagonal - value * value)

    field_terms_0 = jnp.einsum(
        "lab,lb->la", ours(sensitivity), ours(leaf_field), preferred_element_type=jnp.float32
    )
    field_terms_2 = jnp.einsum(
        "lab,lb->la", sens_in, ours(leaf_field), preferred_element_type=jnp.float32
    )
    returned_0 = jnp.sum(ours(sensitivity).astype(jnp.float32) * cross_0, 2) - taken[
        :, 0, share, :share
    ].astype(jnp.float32) * field_terms_0
    returned_2 = jnp.sum(sens_in.astype(jnp.float32) * cross_2, 2) - taken[
        :, 1, share, :share
    ].astype(jnp.float32) * field_terms_2
    owners = (
        parent_ids[:, None] == lax.broadcasted_iota(jnp.int32, (owned, number), 1)
    ).astype(jnp.float32)
    spread_0 = jnp.einsum("lp,la->pa", owners, returned_0, precision=lax.Precision.HIGHEST)
    spread_2 = jnp.einsum("lp,la->pa", owners, returned_2, precision=lax.Precision.HIGHEST)
    spread = spread_0 + far(spread_2)
    coupling_grad = reduce_to_owner(spread, me_leaf, number)
    return (leaf_grad, coupling_grad)


def solution(mesh):
    in_specs = (
        P("leaf", None, "blk"),
        P("leaf", "blk", None),
        P("leaf", "blk", None),
        P("leaf", "blk", None),
        P("leaf", None),
        P("leaf", None),
        P("leaf", "blk"),
    )
    out_specs = (P("leaf", "blk"), P("leaf", "blk"))
    return jax.shard_map(body, mesh=mesh, in_specs=in_specs, out_specs=out_specs, check_vma=False)
```

```python
import jax
import jax.numpy as jnp
from jax import lax
from jax.sharding import PartitionSpec as P


def swap(x, axis, mask):
    size = lax.axis_size(axis)
    return lax.ppermute(x, axis, [(i, i ^ mask) for i in range(size)])


def far(x):
    return swap(x, "blk", 2)


def near(x, far_x):
    both = swap(jnp.stack([x, far_x]), "blk", 1)
    return [x, both[0], far_x, both[1]]


def shift(x, axis, step):
    size = lax.axis_size(axis)
    return lax.ppermute(x, axis, [(i, (i + step) % size) for i in range(size)])


def tied(*values):
    return lax.optimization_barrier(values)


def reduce_to_owner(spread, me, number):
    if number & (number - 1):
        total = lax.dynamic_slice_in_dim(spread, me, 1, 0)
        for s in range(1, number):
            row = lax.dynamic_slice_in_dim(spread, (me + s) % number, 1, 0)
            total = total + shift(row, "leaf", s)
        return total
    current = spread
    mask = 1
    while mask < number:
        bit = (me & mask) // mask
        pairs = current.reshape(current.shape[0] // 2, 2, current.shape[1])
        keep = lax.dynamic_index_in_dim(pairs, bit, 1, keepdims=False)
        give = lax.dynamic_index_in_dim(pairs, 1 - bit, 1, keepdims=False)
        current = keep + swap(give, "leaf", mask)
        mask *= 2
    return current


def body(parent_inverse, leaf_inverse, coupling, sensitivity, parent_of, leaf_field, parent_field):
    count, share, width = coupling.shape
    me_blk = lax.axis_index("blk")
    me_leaf = lax.axis_index("leaf")
    number = lax.axis_size("leaf")
    offset = me_blk * share
    owned = count // 2
    chip = me_blk >> 1
    mine_at = chip * owned
    theirs_at = (1 - chip) * owned

    def by_blocks(left, blocks):
        cols = jnp.concatenate(
            [lax.dynamic_slice_in_dim(left, (me_blk ^ t) * share, share, 2) for t in range(len(blocks))],
            axis=2,
        )
        right = jnp.concatenate(blocks, axis=1)
        return jnp.einsum("lik,lkc->lic", cols, right, preferred_element_type=jnp.float32)

    def ours(x):
        return lax.dynamic_slice_in_dim(x, mine_at, owned, 0)

    def theirs(x):
        return lax.dynamic_slice_in_dim(x, theirs_at, owned, 0)

    upper_far = far(jnp.concatenate([parent_inverse, parent_field[:, None, :]], axis=1))
    outgoing, upper_far = tied(
        jnp.stack([theirs(coupling), theirs(leaf_inverse), theirs(sensitivity)]), upper_far
    )
    incoming = far(outgoing)
    field_far = upper_far[:, width, :]
    upper_far = upper_far[:, :width, :]
    upper_blocks = near(parent_inverse, upper_far)
    upper = jnp.take(jnp.stack(upper_blocks), jnp.arange(4) ^ me_blk, axis=0)
    upper = jnp.concatenate([upper[t] for t in range(4)], axis=2)

    def packed_rows(columns, field):
        rows = jnp.einsum(
            "pkr,pkc->prc", columns, upper, preferred_element_type=jnp.float32
        ).astype(jnp.bfloat16)
        field_row = jnp.pad(field, ((0, 0), (0, width - share)))[:, None, :]
        return jnp.concatenate([rows, field_row], axis=1)[0]

    packed = jnp.stack([packed_rows(parent_inverse, parent_field), packed_rows(upper_far, field_far)])
    pieces = jnp.stack([packed] + [shift(packed, "leaf", s) for s in range(1, number)])

    incoming, pieces = tied(incoming, pieces)
    sens_in = incoming[2]
    coupling_0, coupling_2 = ours(coupling), incoming[0]
    inverse_0, inverse_2 = ours(leaf_inverse), incoming[1]
    inverse_blocks = near(inverse_0, inverse_2)
    product_0 = by_blocks(coupling_0, inverse_blocks)
    product_2 = by_blocks(coupling_2, inverse_blocks)
    mixed_blocks = near(product_0.astype(jnp.bfloat16), product_2.astype(jnp.bfloat16))

    parent_ids = ours(parent_of)[:, 0]
    clipped = jnp.clip(parent_ids, 0, number - 1)
    position = (me_leaf - clipped) % number
    taken = jnp.take(pieces, position, axis=0)
    cross_0 = -by_blocks(taken[:, 0, :share, :], mixed_blocks)
    cross_2 = -by_blocks(taken[:, 1, :share, :], mixed_blocks)

    def diag_part(inverse_t, cross_t, product_t):
        factor = inverse_t.astype(jnp.float32)
        return jnp.sum(factor * factor, 1) - jnp.sum(
            cross_t.astype(jnp.bfloat16).astype(jnp.float32) * product_t, 1
        )

    partial_diag = diag_part(inverse_0, cross_0, product_0) + diag_part(inverse_2, cross_2, product_2)
    full_diag = partial_diag + swap(partial_diag, "blk", 1)
    own_cols = lax.dynamic_slice_in_dim(full_diag, offset, share, 1)
    their_cols = far(lax.dynamic_slice_in_dim(full_diag, (me_blk ^ 2) * share, share, 1))
    diagonal = jnp.where(
        chip == 0,
        jnp.concatenate([own_cols, their_cols], axis=0),
        jnp.concatenate([their_cols, own_cols], axis=0),
    )
    value = lax.dynamic_slice_in_dim(leaf_field, offset, share, 1).astype(jnp.float32)
    leaf_grad = 0.5 * (diagonal - value * value)

    field_terms_0 = jnp.einsum(
        "lab,lb->la", ours(sensitivity), ours(leaf_field), preferred_element_type=jnp.float32
    )
    field_terms_2 = jnp.einsum(
        "lab,lb->la", sens_in, ours(leaf_field), preferred_element_type=jnp.float32
    )
    returned_0 = jnp.sum(ours(sensitivity).astype(jnp.float32) * cross_0, 2) - taken[
        :, 0, share, :share
    ].astype(jnp.float32) * field_terms_0
    returned_2 = jnp.sum(sens_in.astype(jnp.float32) * cross_2, 2) - taken[
        :, 1, share, :share
    ].astype(jnp.float32) * field_terms_2
    owners = (
        parent_ids[:, None] == lax.broadcasted_iota(jnp.int32, (owned, number), 1)
    ).astype(jnp.float32)
    spread_0 = jnp.einsum("lp,la->pa", owners, returned_0, precision=lax.Precision.HIGHEST)
    spread_2 = jnp.einsum("lp,la->pa", owners, returned_2, precision=lax.Precision.HIGHEST)
    spread = spread_0 + far(spread_2)
    coupling_grad = reduce_to_owner(spread, me_leaf, number)
    return (leaf_grad, coupling_grad)


def solution(mesh):
    in_specs = (
        P("leaf", None, "blk"),
        P("leaf", "blk", None),
        P("leaf", "blk", None),
        P("leaf", "blk", None),
        P("leaf", None),
        P("leaf", None),
        P("leaf", "blk"),
    )
    out_specs = (P("leaf", "blk"), P("leaf", "blk"))
    return jax.shard_map(body, mesh=mesh, in_specs=in_specs, out_specs=out_specs, check_vma=False)
```

```python
import jax
import jax.numpy as jnp
from jax import lax
from jax.sharding import PartitionSpec as P


def swap(x, axis, mask):
    size = lax.axis_size(axis)
    return lax.ppermute(x, axis, [(i, i ^ mask) for i in range(size)])


def far(x):
    return swap(x, "blk", 2)


def near(x, far_x):
    both = swap(jnp.stack([x, far_x]), "blk", 1)
    return [x, both[0], far_x, both[1]]


def shift(x, axis, step):
    size = lax.axis_size(axis)
    return lax.ppermute(x, axis, [(i, (i + step) % size) for i in range(size)])


def tied(*values):
    return lax.optimization_barrier(values)


def reduce_to_owner(spread, me, number):
    if number & (number - 1):
        total = lax.dynamic_slice_in_dim(spread, me, 1, 0)
        for s in range(1, number):
            row = lax.dynamic_slice_in_dim(spread, (me + s) % number, 1, 0)
            total = total + shift(row, "leaf", s)
        return total
    current = spread
    mask = 1
    while mask < number:
        bit = (me & mask) // mask
        pairs = current.reshape(current.shape[0] // 2, 2, current.shape[1])
        keep = lax.dynamic_index_in_dim(pairs, bit, 1, keepdims=False)
        give = lax.dynamic_index_in_dim(pairs, 1 - bit, 1, keepdims=False)
        current = keep + swap(give, "leaf", mask)
        mask *= 2
    return current


def body(parent_inverse, leaf_inverse, coupling, sensitivity, parent_of, leaf_field, parent_field):
    count, share, width = coupling.shape
    me_blk = lax.axis_index("blk")
    me_leaf = lax.axis_index("leaf")
    number = lax.axis_size("leaf")
    offset = me_blk * share
    owned = count // 2
    chip = me_blk >> 1
    mine_at = chip * owned
    theirs_at = (1 - chip) * owned

    def by_blocks(left, blocks):
        cols = jnp.concatenate(
            [lax.dynamic_slice_in_dim(left, (me_blk ^ t) * share, share, 2) for t in range(len(blocks))],
            axis=2,
        )
        right = jnp.concatenate(blocks, axis=1)
        return jnp.einsum("lik,lkc->lic", cols, right, preferred_element_type=jnp.float32)

    def ours(x):
        return lax.dynamic_slice_in_dim(x, mine_at, owned, 0)

    def theirs(x):
        return lax.dynamic_slice_in_dim(x, theirs_at, owned, 0)

    upper_far = far(jnp.concatenate([parent_inverse, parent_field[:, None, :]], axis=1))
    outgoing, upper_far = tied(
        jnp.stack([theirs(coupling), theirs(leaf_inverse), theirs(sensitivity)]), upper_far
    )
    incoming = far(outgoing)
    field_far = upper_far[:, width, :]
    upper_far = upper_far[:, :width, :]
    upper_blocks = near(parent_inverse, upper_far)
    upper = jnp.take(jnp.stack(upper_blocks), jnp.arange(4) ^ me_blk, axis=0)
    upper = jnp.concatenate([upper[t] for t in range(4)], axis=2)

    def packed_rows(columns, field):
        rows = jnp.einsum(
            "pkr,pkc->prc", columns, upper, preferred_element_type=jnp.float32
        ).astype(jnp.bfloat16)
        field_row = jnp.pad(field, ((0, 0), (0, width - share)))[:, None, :]
        return jnp.concatenate([rows, field_row], axis=1)[0]

    packed = jnp.stack([packed_rows(parent_inverse, parent_field), packed_rows(upper_far, field_far)])
    pieces = jnp.stack([packed] + [shift(packed, "leaf", s) for s in range(1, number)])

    incoming, pieces = tied(incoming, pieces)
    sens_in = incoming[2]
    coupling_0, coupling_2 = ours(coupling), incoming[0]
    inverse_0, inverse_2 = ours(leaf_inverse), incoming[1]
    inverse_blocks = near(inverse_0, inverse_2)
    product_0 = by_blocks(coupling_0, inverse_blocks)
    product_2 = by_blocks(coupling_2, inverse_blocks)
    mixed_blocks = near(product_0.astype(jnp.bfloat16), product_2.astype(jnp.bfloat16))

    parent_ids = ours(parent_of)[:, 0]
    clipped = jnp.clip(parent_ids, 0, number - 1)
    position = (me_leaf - clipped) % number
    taken = jnp.take(pieces, position, axis=0)
    cross_0 = -by_blocks(taken[:, 0, :share, :], mixed_blocks)
    cross_2 = -by_blocks(taken[:, 1, :share, :], mixed_blocks)

    def diag_part(inverse_t, cross_t, product_t):
        factor = inverse_t.astype(jnp.float32)
        return jnp.sum(factor * factor, 1) - jnp.sum(
            cross_t.astype(jnp.bfloat16).astype(jnp.float32) * product_t, 1
        )

    partial_diag = diag_part(inverse_0, cross_0, product_0) + diag_part(inverse_2, cross_2, product_2)
    full_diag = partial_diag + swap(partial_diag, "blk", 1)
    own_cols = lax.dynamic_slice_in_dim(full_diag, offset, share, 1)
    their_cols_out = lax.dynamic_slice_in_dim(full_diag, (me_blk ^ 2) * share, share, 1)
    field_terms_0 = jnp.einsum(
        "lab,lb->la", ours(sensitivity), ours(leaf_field), preferred_element_type=jnp.float32
    )
    field_terms_2 = jnp.einsum(
        "lab,lb->la", sens_in, ours(leaf_field), preferred_element_type=jnp.float32
    )
    returned_0 = jnp.sum(ours(sensitivity).astype(jnp.float32) * cross_0, 2) - taken[
        :, 0, share, :share
    ].astype(jnp.float32) * field_terms_0
    returned_2 = jnp.sum(sens_in.astype(jnp.float32) * cross_2, 2) - taken[
        :, 1, share, :share
    ].astype(jnp.float32) * field_terms_2
    owners = (
        parent_ids[:, None] == lax.broadcasted_iota(jnp.int32, (owned, number), 1)
    ).astype(jnp.float32)
    spread_0 = jnp.einsum("lp,la->pa", owners, returned_0, precision=lax.Precision.HIGHEST)
    spread_2 = jnp.einsum("lp,la->pa", owners, returned_2, precision=lax.Precision.HIGHEST)
    across = far(jnp.concatenate([their_cols_out, spread_2], axis=0))
    their_cols = across[:owned]
    spread = spread_0 + across[owned:]
    diagonal = jnp.where(
        chip == 0,
        jnp.concatenate([own_cols, their_cols], axis=0),
        jnp.concatenate([their_cols, own_cols], axis=0),
    )
    value = lax.dynamic_slice_in_dim(leaf_field, offset, share, 1).astype(jnp.float32)
    leaf_grad = 0.5 * (diagonal - value * value)

    coupling_grad = reduce_to_owner(spread, me_leaf, number)
    return (leaf_grad, coupling_grad)


def solution(mesh):
    in_specs = (
        P("leaf", None, "blk"),
        P("leaf", "blk", None),
        P("leaf", "blk", None),
        P("leaf", "blk", None),
        P("leaf", None),
        P("leaf", None),
        P("leaf", "blk"),
    )
    out_specs = (P("leaf", "blk"), P("leaf", "blk"))
    return jax.shard_map(body, mesh=mesh, in_specs=in_specs, out_specs=out_specs, check_vma=False)
```

```python
import jax
import jax.numpy as jnp
from jax import lax
from jax.sharding import PartitionSpec as P


def swap(x, axis, mask):
    size = lax.axis_size(axis)
    return lax.ppermute(x, axis, [(i, i ^ mask) for i in range(size)])


def far(x):
    return swap(x, "blk", 2)


def near(x, far_x):
    both = swap(jnp.stack([x, far_x]), "blk", 1)
    return [x, both[0], far_x, both[1]]


def shift(x, axis, step):
    size = lax.axis_size(axis)
    return lax.ppermute(x, axis, [(i, (i + step) % size) for i in range(size)])


def tied(*values):
    return lax.optimization_barrier(values)


def reduce_to_owner(spread, me, number):
    if number & (number - 1):
        total = lax.dynamic_slice_in_dim(spread, me, 1, 0)
        for s in range(1, number):
            row = lax.dynamic_slice_in_dim(spread, (me + s) % number, 1, 0)
            total = total + shift(row, "leaf", s)
        return total
    current = spread
    mask = 1
    while mask < number:
        bit = (me & mask) // mask
        pairs = current.reshape(current.shape[0] // 2, 2, current.shape[1])
        keep = lax.dynamic_index_in_dim(pairs, bit, 1, keepdims=False)
        give = lax.dynamic_index_in_dim(pairs, 1 - bit, 1, keepdims=False)
        current = keep + swap(give, "leaf", mask)
        mask *= 2
    return current


def body(parent_inverse, leaf_inverse, coupling, sensitivity, parent_of, leaf_field, parent_field):
    count, share, width = coupling.shape
    me_blk = lax.axis_index("blk")
    me_leaf = lax.axis_index("leaf")
    number = lax.axis_size("leaf")
    offset = me_blk * share
    owned = count // 2
    chip = me_blk >> 1
    mine_at = chip * owned
    theirs_at = (1 - chip) * owned

    def by_blocks(left, blocks):
        cols = jnp.concatenate(
            [lax.dynamic_slice_in_dim(left, (me_blk ^ t) * share, share, 2) for t in range(len(blocks))],
            axis=2,
        )
        right = jnp.concatenate(blocks, axis=1)
        return jnp.einsum("lik,lkc->lic", cols, right, preferred_element_type=jnp.float32)

    def ours(x):
        return lax.dynamic_slice_in_dim(x, mine_at, owned, 0)

    def theirs(x):
        return lax.dynamic_slice_in_dim(x, theirs_at, owned, 0)

    upper_far = far(jnp.concatenate([parent_inverse, parent_field[:, None, :]], axis=1))
    outgoing, upper_far = tied(
        jnp.stack([theirs(coupling), theirs(leaf_inverse), theirs(sensitivity)]), upper_far
    )
    split = (owned + 1) // 2
    incoming_a = far(outgoing[:, :split])
    field_far = upper_far[:, width, :]
    upper_far = upper_far[:, :width, :]
    upper_blocks = near(parent_inverse, upper_far)
    upper = jnp.take(jnp.stack(upper_blocks), jnp.arange(4) ^ me_blk, axis=0)
    upper = jnp.concatenate([upper[t] for t in range(4)], axis=2)

    def packed_rows(columns, field):
        rows = jnp.einsum(
            "pkr,pkc->prc", columns, upper, preferred_element_type=jnp.float32
        ).astype(jnp.bfloat16)
        field_row = jnp.pad(field, ((0, 0), (0, width - share)))[:, None, :]
        return jnp.concatenate([rows, field_row], axis=1)[0]

    packed = jnp.stack([packed_rows(parent_inverse, parent_field), packed_rows(upper_far, field_far)])
    pieces = jnp.stack([packed] + [shift(packed, "leaf", s) for s in range(1, number)])

    incoming_a, pieces = tied(incoming_a, pieces)
    outgoing_b, incoming_a = tied(outgoing[:, split:], incoming_a)
    incoming_b = far(outgoing_b)
    parent_ids = ours(parent_of)[:, 0]
    clipped = jnp.clip(parent_ids, 0, number - 1)
    position = (me_leaf - clipped) % number
    taken = jnp.take(pieces, position, axis=0)

    def diag_part(inverse_t, cross_t, product_t):
        factor = inverse_t.astype(jnp.float32)
        return jnp.sum(factor * factor, 1) - jnp.sum(
            cross_t.astype(jnp.bfloat16).astype(jnp.float32) * product_t, 1
        )

    def chunk(part, incoming):
        coupling_0, coupling_2 = ours(coupling)[part], incoming[0]
        inverse_0, inverse_2 = ours(leaf_inverse)[part], incoming[1]
        sens_0, sens_2 = ours(sensitivity)[part], incoming[2]
        inverse_blocks = near(inverse_0, inverse_2)
        product_0 = by_blocks(coupling_0, inverse_blocks)
        product_2 = by_blocks(coupling_2, inverse_blocks)
        mixed_blocks = near(product_0.astype(jnp.bfloat16), product_2.astype(jnp.bfloat16))
        local = taken[part]
        cross_0 = -by_blocks(local[:, 0, :share, :], mixed_blocks)
        cross_2 = -by_blocks(local[:, 1, :share, :], mixed_blocks)
        partial = diag_part(inverse_0, cross_0, product_0) + diag_part(inverse_2, cross_2, product_2)
        field = ours(leaf_field)[part]
        terms_0 = jnp.einsum("lab,lb->la", sens_0, field, preferred_element_type=jnp.float32)
        terms_2 = jnp.einsum("lab,lb->la", sens_2, field, preferred_element_type=jnp.float32)
        returned_0 = jnp.sum(sens_0.astype(jnp.float32) * cross_0, 2) - local[
            :, 0, share, :share
        ].astype(jnp.float32) * terms_0
        returned_2 = jnp.sum(sens_2.astype(jnp.float32) * cross_2, 2) - local[
            :, 1, share, :share
        ].astype(jnp.float32) * terms_2
        return partial, returned_0, returned_2

    first = chunk(slice(0, split), incoming_a)
    second = chunk(slice(split, owned), incoming_b)
    partial_diag, returned_0, returned_2 = [
        jnp.concatenate([x, y], axis=0) for x, y in zip(first, second)
    ]
    full_diag = partial_diag + swap(partial_diag, "blk", 1)
    own_cols = lax.dynamic_slice_in_dim(full_diag, offset, share, 1)
    their_cols_out = lax.dynamic_slice_in_dim(full_diag, (me_blk ^ 2) * share, share, 1)
    owners = (
        parent_ids[:, None] == lax.broadcasted_iota(jnp.int32, (owned, number), 1)
    ).astype(jnp.float32)
    spread_0 = jnp.einsum("lp,la->pa", owners, returned_0, precision=lax.Precision.HIGHEST)
    spread_2 = jnp.einsum("lp,la->pa", owners, returned_2, precision=lax.Precision.HIGHEST)
    across = far(jnp.concatenate([their_cols_out, spread_2], axis=0))
    their_cols = across[:owned]
    spread = spread_0 + across[owned:]
    diagonal = jnp.where(
        chip == 0,
        jnp.concatenate([own_cols, their_cols], axis=0),
        jnp.concatenate([their_cols, own_cols], axis=0),
    )
    value = lax.dynamic_slice_in_dim(leaf_field, offset, share, 1).astype(jnp.float32)
    leaf_grad = 0.5 * (diagonal - value * value)

    coupling_grad = reduce_to_owner(spread, me_leaf, number)
    return (leaf_grad, coupling_grad)


def solution(mesh):
    in_specs = (
        P("leaf", None, "blk"),
        P("leaf", "blk", None),
        P("leaf", "blk", None),
        P("leaf", "blk", None),
        P("leaf", None),
        P("leaf", None),
        P("leaf", "blk"),
    )
    out_specs = (P("leaf", "blk"), P("leaf", "blk"))
    return jax.shard_map(body, mesh=mesh, in_specs=in_specs, out_specs=out_specs, check_vma=False)
```

```python
import jax
import jax.numpy as jnp
from jax import lax
from jax.sharding import PartitionSpec as P


def swap(x, axis, mask):
    size = lax.axis_size(axis)
    return lax.ppermute(x, axis, [(i, i ^ mask) for i in range(size)])


def far(x):
    return swap(x, "blk", 2)


def near(x, far_x):
    both = swap(jnp.stack([x, far_x]), "blk", 1)
    return [x, both[0], far_x, both[1]]


def shift(x, axis, step):
    size = lax.axis_size(axis)
    return lax.ppermute(x, axis, [(i, (i + step) % size) for i in range(size)])


def tied(*values):
    return lax.optimization_barrier(values)


def reduce_to_owner(spread, me, number):
    if number & (number - 1):
        total = lax.dynamic_slice_in_dim(spread, me, 1, 0)
        for s in range(1, number):
            row = lax.dynamic_slice_in_dim(spread, (me + s) % number, 1, 0)
            total = total + shift(row, "leaf", s)
        return total
    current = spread
    mask = 1
    while mask < number:
        bit = (me & mask) // mask
        pairs = current.reshape(current.shape[0] // 2, 2, current.shape[1])
        keep = lax.dynamic_index_in_dim(pairs, bit, 1, keepdims=False)
        give = lax.dynamic_index_in_dim(pairs, 1 - bit, 1, keepdims=False)
        current = keep + swap(give, "leaf", mask)
        mask *= 2
    return current


def body(parent_inverse, leaf_inverse, coupling, sensitivity, parent_of, leaf_field, parent_field):
    count, share, width = coupling.shape
    me_blk = lax.axis_index("blk")
    me_leaf = lax.axis_index("leaf")
    number = lax.axis_size("leaf")
    offset = me_blk * share
    owned = count // 2
    chip = me_blk >> 1
    mine_at = chip * owned
    theirs_at = (1 - chip) * owned

    def by_blocks(left, blocks):
        cols = jnp.concatenate(
            [lax.dynamic_slice_in_dim(left, (me_blk ^ t) * share, share, 2) for t in range(len(blocks))],
            axis=2,
        )
        right = jnp.concatenate(blocks, axis=1)
        return jnp.einsum("lik,lkc->lic", cols, right, preferred_element_type=jnp.float32)

    def ours(x):
        return lax.dynamic_slice_in_dim(x, mine_at, owned, 0)

    def theirs(x):
        return lax.dynamic_slice_in_dim(x, theirs_at, owned, 0)

    upper_far = far(jnp.concatenate([parent_inverse, parent_field[:, None, :]], axis=1))
    outgoing, upper_far = tied(
        jnp.stack([theirs(coupling), theirs(leaf_inverse), theirs(sensitivity)]), upper_far
    )
    incoming = far(outgoing)
    field_far = upper_far[:, width, :]
    upper_far = upper_far[:, :width, :]
    upper_blocks = near(parent_inverse, upper_far)
    upper = jnp.take(jnp.stack(upper_blocks), jnp.arange(4) ^ me_blk, axis=0)
    upper = jnp.concatenate([upper[t] for t in range(4)], axis=2)

    def packed_rows(columns, field):
        rows = jnp.einsum(
            "pkr,pkc->prc", columns, upper, preferred_element_type=jnp.float32
        ).astype(jnp.bfloat16)
        field_row = jnp.pad(field, ((0, 0), (0, width - share)))[:, None, :]
        return jnp.concatenate([rows, field_row], axis=1)[0]

    packed = jnp.stack([packed_rows(parent_inverse, parent_field), packed_rows(upper_far, field_far)])
    pieces = jnp.stack([packed] + [shift(packed, "leaf", s) for s in range(1, number)])

    parent_ids = ours(parent_of)[:, 0]
    clipped = jnp.clip(parent_ids, 0, number - 1)
    position = (me_leaf - clipped) % number
    taken = jnp.take(pieces, position, axis=0)
    incoming, taken, own_coupling, own_inverse, own_sens = tied(
        incoming, taken, ours(coupling), ours(leaf_inverse), ours(sensitivity)
    )
    sens_in = incoming[2]
    coupling_0, coupling_2 = own_coupling, incoming[0]
    inverse_0, inverse_2 = own_inverse, incoming[1]
    inverse_blocks = near(inverse_0, inverse_2)
    product_0 = by_blocks(coupling_0, inverse_blocks)
    product_2 = by_blocks(coupling_2, inverse_blocks)
    mixed_blocks = near(product_0.astype(jnp.bfloat16), product_2.astype(jnp.bfloat16))

    cross_0 = -by_blocks(taken[:, 0, :share, :], mixed_blocks)
    cross_2 = -by_blocks(taken[:, 1, :share, :], mixed_blocks)

    def diag_part(inverse_t, cross_t, product_t):
        factor = inverse_t.astype(jnp.float32)
        return jnp.sum(factor * factor, 1) - jnp.sum(
            cross_t.astype(jnp.bfloat16).astype(jnp.float32) * product_t, 1
        )

    partial_diag = diag_part(inverse_0, cross_0, product_0) + diag_part(inverse_2, cross_2, product_2)
    full_diag = partial_diag + swap(partial_diag, "blk", 1)
    own_cols = lax.dynamic_slice_in_dim(full_diag, offset, share, 1)
    their_cols = far(lax.dynamic_slice_in_dim(full_diag, (me_blk ^ 2) * share, share, 1))
    diagonal = jnp.where(
        chip == 0,
        jnp.concatenate([own_cols, their_cols], axis=0),
        jnp.concatenate([their_cols, own_cols], axis=0),
    )
    value = lax.dynamic_slice_in_dim(leaf_field, offset, share, 1).astype(jnp.float32)
    leaf_grad = 0.5 * (diagonal - value * value)

    field_terms_0 = jnp.einsum(
        "lab,lb->la", own_sens, ours(leaf_field), preferred_element_type=jnp.float32
    )
    field_terms_2 = jnp.einsum(
        "lab,lb->la", sens_in, ours(leaf_field), preferred_element_type=jnp.float32
    )
    returned_0 = jnp.sum(own_sens.astype(jnp.float32) * cross_0, 2) - taken[
        :, 0, share, :share
    ].astype(jnp.float32) * field_terms_0
    returned_2 = jnp.sum(sens_in.astype(jnp.float32) * cross_2, 2) - taken[
        :, 1, share, :share
    ].astype(jnp.float32) * field_terms_2
    owners = (
        parent_ids[:, None] == lax.broadcasted_iota(jnp.int32, (owned, number), 1)
    ).astype(jnp.float32)
    spread_0 = jnp.einsum("lp,la->pa", owners, returned_0, precision=lax.Precision.HIGHEST)
    spread_2 = jnp.einsum("lp,la->pa", owners, returned_2, precision=lax.Precision.HIGHEST)
    spread = spread_0 + far(spread_2)
    coupling_grad = reduce_to_owner(spread, me_leaf, number)
    return (leaf_grad, coupling_grad)


def solution(mesh):
    in_specs = (
        P("leaf", None, "blk"),
        P("leaf", "blk", None),
        P("leaf", "blk", None),
        P("leaf", "blk", None),
        P("leaf", None),
        P("leaf", None),
        P("leaf", "blk"),
    )
    out_specs = (P("leaf", "blk"), P("leaf", "blk"))
    return jax.shard_map(body, mesh=mesh, in_specs=in_specs, out_specs=out_specs, check_vma=False)
```

```python
import jax
import jax.numpy as jnp
from jax import lax
from jax.sharding import PartitionSpec as P


def swap(x, axis, mask):
    size = lax.axis_size(axis)
    return lax.ppermute(x, axis, [(i, i ^ mask) for i in range(size)])


def far(x):
    return swap(x, "blk", 2)


def near(x, far_x):
    both = swap(jnp.stack([x, far_x]), "blk", 1)
    return [x, both[0], far_x, both[1]]


def shift(x, axis, step):
    size = lax.axis_size(axis)
    return lax.ppermute(x, axis, [(i, (i + step) % size) for i in range(size)])


def tied(*values):
    return lax.optimization_barrier(values)


def reduce_to_owner(spread, me, number):
    if number & (number - 1):
        total = lax.dynamic_slice_in_dim(spread, me, 1, 0)
        for s in range(1, number):
            row = lax.dynamic_slice_in_dim(spread, (me + s) % number, 1, 0)
            total = total + shift(row, "leaf", s)
        return total
    current = spread
    mask = 1
    while mask < number:
        bit = (me & mask) // mask
        pairs = current.reshape(current.shape[0] // 2, 2, current.shape[1])
        keep = lax.dynamic_index_in_dim(pairs, bit, 1, keepdims=False)
        give = lax.dynamic_index_in_dim(pairs, 1 - bit, 1, keepdims=False)
        current = keep + swap(give, "leaf", mask)
        mask *= 2
    return current


def body(parent_inverse, leaf_inverse, coupling, sensitivity, parent_of, leaf_field, parent_field):
    count, share, width = coupling.shape
    me_blk = lax.axis_index("blk")
    me_leaf = lax.axis_index("leaf")
    number = lax.axis_size("leaf")
    offset = me_blk * share
    owned = count // 2
    chip = me_blk >> 1
    mine_at = chip * owned
    theirs_at = (1 - chip) * owned

    def by_blocks(left, blocks):
        cols = jnp.concatenate(
            [lax.dynamic_slice_in_dim(left, (me_blk ^ t) * share, share, 2) for t in range(len(blocks))],
            axis=2,
        )
        right = jnp.concatenate(blocks, axis=1)
        return jnp.einsum("lik,lkc->lic", cols, right, preferred_element_type=jnp.float32)

    def ours(x):
        return lax.dynamic_slice_in_dim(x, mine_at, owned, 0)

    def theirs(x):
        return lax.dynamic_slice_in_dim(x, theirs_at, owned, 0)

    upper_far = far(jnp.concatenate([parent_inverse, parent_field[:, None, :]], axis=1))
    outgoing, upper_far = tied(
        jnp.stack([theirs(coupling), theirs(leaf_inverse), theirs(sensitivity)]), upper_far
    )
    incoming = far(outgoing)
    field_far = upper_far[:, width, :]
    upper_far = upper_far[:, :width, :]
    upper_blocks = near(parent_inverse, upper_far)
    upper = jnp.take(jnp.stack(upper_blocks), jnp.arange(4) ^ me_blk, axis=0)
    upper = jnp.concatenate([upper[t] for t in range(4)], axis=2)

    def packed_rows(columns, field):
        rows = jnp.einsum(
            "pkr,pkc->prc", columns, upper, preferred_element_type=jnp.float32
        ).astype(jnp.bfloat16)
        field_row = jnp.pad(field, ((0, 0), (0, width - share)))[:, None, :]
        return jnp.concatenate([rows, field_row], axis=1)[0]

    packed = jnp.stack([packed_rows(parent_inverse, parent_field), packed_rows(upper_far, field_far)])
    pieces = jnp.stack([packed] + [shift(packed, "leaf", s) for s in range(1, number)])

    parent_ids = ours(parent_of)[:, 0]
    clipped = jnp.clip(parent_ids, 0, number - 1)
    position = (me_leaf - clipped) % number
    incoming, taken = tied(incoming, jnp.take(pieces, position, axis=0))
    sens_in = incoming[2]
    coupling_0, coupling_2 = ours(coupling), incoming[0]
    inverse_0, inverse_2 = ours(leaf_inverse), incoming[1]
    inverse_blocks = near(inverse_0, inverse_2)
    product_0 = by_blocks(coupling_0, inverse_blocks)
    product_2 = by_blocks(coupling_2, inverse_blocks)
    mixed_blocks = near(product_0.astype(jnp.bfloat16), product_2.astype(jnp.bfloat16))

    cross_0 = -by_blocks(taken[:, 0, :share, :], mixed_blocks)
    cross_2 = -by_blocks(taken[:, 1, :share, :], mixed_blocks)

    def diag_part(inverse_t, cross_t, product_t):
        factor = inverse_t.astype(jnp.float32)
        return jnp.sum(factor * factor, 1) - jnp.sum(
            cross_t.astype(jnp.bfloat16).astype(jnp.float32) * product_t, 1
        )

    partial_diag = diag_part(inverse_0, cross_0, product_0) + diag_part(inverse_2, cross_2, product_2)
    full_diag = partial_diag + swap(partial_diag, "blk", 1)
    own_cols = lax.dynamic_slice_in_dim(full_diag, offset, share, 1)
    their_cols = far(lax.dynamic_slice_in_dim(full_diag, (me_blk ^ 2) * share, share, 1))
    diagonal = jnp.where(
        chip == 0,
        jnp.concatenate([own_cols, their_cols], axis=0),
        jnp.concatenate([their_cols, own_cols], axis=0),
    )
    value = lax.dynamic_slice_in_dim(leaf_field, offset, share, 1).astype(jnp.float32)
    leaf_grad = 0.5 * (diagonal - value * value)

    field_terms_0 = jnp.einsum(
        "lab,lb->la", ours(sensitivity), ours(leaf_field), preferred_element_type=jnp.float32
    )
    field_terms_2 = jnp.einsum(
        "lab,lb->la", sens_in, ours(leaf_field), preferred_element_type=jnp.float32
    )
    returned_0 = jnp.sum(ours(sensitivity).astype(jnp.float32) * cross_0, 2) - taken[
        :, 0, share, :share
    ].astype(jnp.float32) * field_terms_0
    returned_2 = jnp.sum(sens_in.astype(jnp.float32) * cross_2, 2) - taken[
        :, 1, share, :share
    ].astype(jnp.float32) * field_terms_2
    owners = (
        parent_ids[:, None] == lax.broadcasted_iota(jnp.int32, (owned, number), 1)
    ).astype(jnp.float32)
    spread_0 = jnp.einsum("lp,la->pa", owners, returned_0, precision=lax.Precision.HIGHEST)
    spread_2 = jnp.einsum("lp,la->pa", owners, returned_2, precision=lax.Precision.HIGHEST)
    spread = spread_0 + far(spread_2)
    coupling_grad = reduce_to_owner(spread, me_leaf, number)
    return (leaf_grad, coupling_grad)


def solution(mesh):
    in_specs = (
        P("leaf", None, "blk"),
        P("leaf", "blk", None),
        P("leaf", "blk", None),
        P("leaf", "blk", None),
        P("leaf", None),
        P("leaf", None),
        P("leaf", "blk"),
    )
    out_specs = (P("leaf", "blk"), P("leaf", "blk"))
    return jax.shard_map(body, mesh=mesh, in_specs=in_specs, out_specs=out_specs, check_vma=False)
```

```python
import jax
import jax.numpy as jnp
from jax import lax
from jax.sharding import PartitionSpec as P


def swap(x, axis, mask):
    size = lax.axis_size(axis)
    return lax.ppermute(x, axis, [(i, i ^ mask) for i in range(size)])


def far(x):
    return swap(x, "blk", 2)


def near(x, far_x):
    return [x, swap(x, "blk", 1), far_x, swap(far_x, "blk", 1)]


def shift(x, axis, step):
    size = lax.axis_size(axis)
    return lax.ppermute(x, axis, [(i, (i + step) % size) for i in range(size)])


def tied(*values):
    return lax.optimization_barrier(values)


def reduce_to_owner(spread, me, number):
    if number & (number - 1):
        total = lax.dynamic_slice_in_dim(spread, me, 1, 0)
        for s in range(1, number):
            row = lax.dynamic_slice_in_dim(spread, (me + s) % number, 1, 0)
            total = total + shift(row, "leaf", s)
        return total
    current = spread
    mask = 1
    while mask < number:
        bit = (me & mask) // mask
        pairs = current.reshape(current.shape[0] // 2, 2, current.shape[1])
        keep = lax.dynamic_index_in_dim(pairs, bit, 1, keepdims=False)
        give = lax.dynamic_index_in_dim(pairs, 1 - bit, 1, keepdims=False)
        current = keep + swap(give, "leaf", mask)
        mask *= 2
    return current


def body(parent_inverse, leaf_inverse, coupling, sensitivity, parent_of, leaf_field, parent_field):
    count, share, width = coupling.shape
    me_blk = lax.axis_index("blk")
    me_leaf = lax.axis_index("leaf")
    number = lax.axis_size("leaf")
    offset = me_blk * share
    owned = count // 2
    chip = me_blk >> 1
    mine_at = chip * owned
    theirs_at = (1 - chip) * owned

    def by_blocks(left, blocks):
        cols = jnp.concatenate(
            [lax.dynamic_slice_in_dim(left, (me_blk ^ t) * share, share, 2) for t in range(len(blocks))],
            axis=2,
        )
        right = jnp.concatenate(blocks, axis=1)
        return jnp.einsum("lik,lkc->lic", cols, right, preferred_element_type=jnp.float32)

    def ours(x):
        return lax.dynamic_slice_in_dim(x, mine_at, owned, 0)

    def theirs(x):
        return lax.dynamic_slice_in_dim(x, theirs_at, owned, 0)

    upper_far = far(jnp.concatenate([parent_inverse, parent_field[:, None, :]], axis=1))
    outgoing, upper_far = tied(
        jnp.stack([theirs(coupling), theirs(leaf_inverse), theirs(sensitivity)]), upper_far
    )
    incoming = far(outgoing)
    field_far = upper_far[:, width, :]
    upper_far = upper_far[:, :width, :]
    upper_blocks = near(parent_inverse, upper_far)
    upper = jnp.take(jnp.stack(upper_blocks), jnp.arange(4) ^ me_blk, axis=0)
    upper = jnp.concatenate([upper[t] for t in range(4)], axis=2)

    def packed_rows(columns, field):
        rows = jnp.einsum(
            "pkr,pkc->prc", columns, upper, preferred_element_type=jnp.float32
        ).astype(jnp.bfloat16)
        field_row = jnp.pad(field, ((0, 0), (0, width - share)))[:, None, :]
        return jnp.concatenate([rows, field_row], axis=1)[0]

    packed = jnp.stack([packed_rows(parent_inverse, parent_field), packed_rows(upper_far, field_far)])
    pieces = jnp.stack([packed] + [shift(packed, "leaf", s) for s in range(1, number)])

    incoming, pieces = tied(incoming, pieces)
    sens_in = incoming[2]
    coupling_0, coupling_2 = ours(coupling), incoming[0]
    inverse_0, inverse_2 = ours(leaf_inverse), incoming[1]
    inverse_blocks = near(inverse_0, inverse_2)
    product_0 = by_blocks(coupling_0, inverse_blocks)
    product_2 = by_blocks(coupling_2, inverse_blocks)
    mixed_blocks = near(product_0.astype(jnp.bfloat16), product_2.astype(jnp.bfloat16))

    parent_ids = ours(parent_of)[:, 0]
    clipped = jnp.clip(parent_ids, 0, number - 1)
    position = (me_leaf - clipped) % number
    taken = jnp.take(pieces, position, axis=0)
    cross_0 = -by_blocks(taken[:, 0, :share, :], mixed_blocks)
    cross_2 = -by_blocks(taken[:, 1, :share, :], mixed_blocks)

    def diag_part(inverse_t, cross_t, product_t):
        factor = inverse_t.astype(jnp.float32)
        return jnp.sum(factor * factor, 1) - jnp.sum(
            cross_t.astype(jnp.bfloat16).astype(jnp.float32) * product_t, 1
        )

    partial_diag = diag_part(inverse_0, cross_0, product_0) + diag_part(inverse_2, cross_2, product_2)
    full_diag = partial_diag + swap(partial_diag, "blk", 1)
    own_cols = lax.dynamic_slice_in_dim(full_diag, offset, share, 1)
    their_cols = far(lax.dynamic_slice_in_dim(full_diag, (me_blk ^ 2) * share, share, 1))
    diagonal = jnp.where(
        chip == 0,
        jnp.concatenate([own_cols, their_cols], axis=0),
        jnp.concatenate([their_cols, own_cols], axis=0),
    )
    value = lax.dynamic_slice_in_dim(leaf_field, offset, share, 1).astype(jnp.float32)
    leaf_grad = 0.5 * (diagonal - value * value)

    field_terms_0 = jnp.einsum(
        "lab,lb->la", ours(sensitivity), ours(leaf_field), preferred_element_type=jnp.float32
    )
    field_terms_2 = jnp.einsum(
        "lab,lb->la", sens_in, ours(leaf_field), preferred_element_type=jnp.float32
    )
    returned_0 = jnp.sum(ours(sensitivity).astype(jnp.float32) * cross_0, 2) - taken[
        :, 0, share, :share
    ].astype(jnp.float32) * field_terms_0
    returned_2 = jnp.sum(sens_in.astype(jnp.float32) * cross_2, 2) - taken[
        :, 1, share, :share
    ].astype(jnp.float32) * field_terms_2
    owners = (
        parent_ids[:, None] == lax.broadcasted_iota(jnp.int32, (owned, number), 1)
    ).astype(jnp.float32)
    spread_0 = jnp.einsum("lp,la->pa", owners, returned_0, precision=lax.Precision.HIGHEST)
    spread_2 = jnp.einsum("lp,la->pa", owners, returned_2, precision=lax.Precision.HIGHEST)
    spread = spread_0 + far(spread_2)
    coupling_grad = reduce_to_owner(spread, me_leaf, number)
    return (leaf_grad, coupling_grad)


def solution(mesh):
    in_specs = (
        P("leaf", None, "blk"),
        P("leaf", "blk", None),
        P("leaf", "blk", None),
        P("leaf", "blk", None),
        P("leaf", None),
        P("leaf", None),
        P("leaf", "blk"),
    )
    out_specs = (P("leaf", "blk"), P("leaf", "blk"))
    return jax.shard_map(body, mesh=mesh, in_specs=in_specs, out_specs=out_specs, check_vma=False)
```
